128 devices in a mesh: dp: 32 (over z, y, core), mp: 4 (over x).
Axes of the slice: x: 4, y: 4, z: 4, core: 2. Of those that a mesh axis runs over, the one named last changes fastest.
Arguments:
- tokens: bfloat16 [57344, 1024], P('dp'), may hold values from -60 to 60
- segment_ids: int32 [57344], P('dp'), may hold values from 0 to 127, as said below
- page_table: int32 [448], P('dp'), may hold values from 0 to 447, as said below
- w_query: bfloat16 [1024, 1024], P('dp', 'mp'), may hold values from -0.1875 to 0.1875
- w_key: bfloat16 [1024, 1024], P('dp', 'mp'), may hold values from -0.1875 to 0.1875
- w_value: bfloat16 [1024, 1024], P('dp', 'mp'), may hold values from -0.1875 to 0.1875
- w_out: bfloat16 [1024, 1024], P('mp', 'dp'), may hold values from -1.5 to 1.5
- w_up: bfloat16 [1024, 4096], P('dp', 'mp'), may hold values from -0.1875 to 0.1875
- w_down: bfloat16 [4096, 1024], P('mp', 'dp'), may hold values from -0.09375 to 0.09375
- gain_first: float32 [1024], replicated, may hold values from 0.1 to 1.9
- shift_first: float32 [1024], replicated, may hold values from -3 to 3
- gain_second: float32 [1024], replicated, may hold values from 0.1 to 1.9
- shift_second: float32 [1024], replicated, may hold values from -3 to 3
Outputs:
- mixed: bfloat16 [57344, 1024], P('dp')
- kv_cache: bfloat16 [57344, 2, 1024], P('dp', None, 'mp')
The draws below stay inside these ranges and needn't reach their ends.
Inputs may be any that keep to these rules, and one draw needn't show every extreme that they name: page_table is a permutation of the page slots. Page p lies on device p // 14 in arrival order and goes to device page_table[p] // 14; from one device at most 1 pages go to one device, and some pair reaches 1. `segment_ids`: tokens with equal ids form one request; after dealing, a request's tokens are consecutive and lie on one device, which holds at most 4 requests.
All inputs are finite; a program needn't handle non-finite values.
Results may differ from the reference program's by a relative error of at most 0.014.
Values may be sent and summed in bfloat16 or wider, within the bound.
No kernel may reach another device: no remote copies, remote signals or barrier semaphores. Data moves between devices by JAX's collectives and lax.ppermute only.
A program may use at most 128 MiB of HBM per device.

```python
import jax
import jax.numpy as jnp
from jax import lax

D = 1024
HEADS = 16
HEAD = 64
FF = 4096
PAGE = 128
PAGES_DEV = 14
REQS_DEV = 4
TOK_DEV = 1792
TOKENS = 57344
NPAGES = 448
N_DP = 32
N_MP = 4


def dealing(key):
    key_table = jax.random.fold_in(key, 11)
    key_slots = jax.random.fold_in(key, 12)
    key_cuts = jax.random.fold_in(key, 13)
    shuffled = jax.random.permutation(key_table, N_DP).astype(jnp.int32)
    every = jnp.arange(N_DP, dtype=jnp.int32)
    marked = (every == N_DP // 2) | (every == 1) | (every == N_DP - 1)
    score = shuffled + N_DP * marked.astype(jnp.int32)
    offsets = jnp.argsort(-score).astype(jnp.int32)
    page_index = jnp.arange(PAGES_DEV, dtype=jnp.int32)
    sources = jnp.arange(N_DP, dtype=jnp.int32)
    target = (sources[:, None] + offsets[page_index % N_DP][None, :]) % N_DP
    orders = jax.vmap(lambda sub_key: jax.random.permutation(sub_key, PAGES_DEV).astype(jnp.int32))(jax.random.split(key_slots, N_DP))
    slots = orders[target, jnp.broadcast_to(page_index[None, :], target.shape)]
    table = (target * PAGES_DEV + slots).reshape(-1).astype(jnp.int32)
    cuts = jnp.sort(jax.random.randint(key_cuts, (N_DP, REQS_DEV - 1), 1, TOK_DEV), axis=1)
    position = jnp.arange(TOK_DEV, dtype=jnp.int32)
    counts = jnp.sum((cuts[:, None, :] <= position[None, :, None]).astype(jnp.int32), axis=2)
    dealt_ids = (sources[:, None] * REQS_DEV + counts).reshape(NPAGES, PAGE)
    arrival_ids = dealt_ids[table].reshape(-1).astype(jnp.int32)
    return (table, arrival_ids)


def draw_page_table(key, part):
    return dealing(key)[0]


def draw_segment_ids(key, part):
    return dealing(key)[1]


def draw_tokens(key, part):
    key_base = jax.random.fold_in(key, 1)
    base = jax.random.normal(key_base, (TOKENS, D), jnp.float32)
    return jnp.clip(base, -60.0, 60.0).astype(jnp.bfloat16)


def level_of(own_key, dims, pieces, least, top_value):
    level, own = 1.0, jax.random.fold_in(own_key, 6)
    for axis_at, parts in pieces:
        steps = jnp.exp(jax.random.uniform(jax.random.fold_in(own, axis_at), (parts,), jnp.float32, least / len(pieces), top_value / len(pieces)))
        level = level * jnp.repeat(steps, dims[axis_at] // parts).reshape([-1 if axis == axis_at else 1 for axis in range(len(dims))])
    return level


def noise(own_key, extent, deviation, limit, cuts=(), held_as=jnp.bfloat16):
    entries = jax.random.normal(own_key, extent, jnp.float32) * deviation
    if len(cuts) > 0:
        entries = level_of(own_key, extent, cuts, -0.22, 0.18) * entries
    return jnp.clip(entries, min=-limit, max=limit).astype(held_as)


def setup_inputs(seed: int = 0) -> dict:
    arg_keys = jax.random.split(jax.random.key(seed), 14)
    tokens = draw_tokens(jax.random.fold_in(arg_keys[13], 71), 0)
    segment_ids = draw_segment_ids(jax.random.fold_in(arg_keys[13], 71), 0)
    page_table = draw_page_table(jax.random.fold_in(arg_keys[13], 71), 0)
    w_query = noise(arg_keys[3], (D, D), D ** -0.5, 0.1875, ((0, 32), (1, 4)))
    w_key = noise(arg_keys[4], (D, D), D ** -0.5, 0.1875, ((0, 32), (1, 4)))
    w_value = noise(arg_keys[5], (D, D), D ** -0.5, 0.1875, ((0, 32), (1, 4)))
    w_out = noise(arg_keys[6], (D, D), (HEAD // 4) ** -0.5, 1.5, ((0, 4), (1, 32)))
    w_up = noise(arg_keys[7], (D, FF), D ** -0.5, 0.1875, ((0, 32), (1, 4)))
    w_down = noise(arg_keys[8], (FF, D), FF ** -0.5, 0.09375, ((0, 4), (1, 32)))
    gain_first = jnp.clip(1.0 + 0.18 * jax.random.normal(arg_keys[9], (D,), jnp.float32), 0.1, 1.9)
    shift_first = noise(arg_keys[10], (D,), 0.5, 3.0, (), jnp.float32)
    gain_second = jnp.clip(1.0 + 0.18 * jax.random.normal(arg_keys[11], (D,), jnp.float32), 0.1, 1.9)
    shift_second = noise(arg_keys[12], (D,), 0.5, 3.0, (), jnp.float32)
    return dict(tokens=tokens, segment_ids=segment_ids, page_table=page_table, w_query=w_query, w_key=w_key, w_value=w_value, w_out=w_out, w_up=w_up, w_down=w_down, gain_first=gain_first, shift_first=shift_first, gain_second=gain_second, shift_second=shift_second)


def layer_norm(hidden_sum, gain, shift):
    center = hidden_sum - lax.optimization_barrier(jnp.mean(hidden_sum, axis=-1, keepdims=True))
    spread = lax.optimization_barrier(jnp.mean(center * center, axis=-1, keepdims=True))
    return center * lax.rsqrt(spread + 1e-05) * gain + shift

def attend_head(query, keys, values, segments):
    scores = jnp.einsum('qd,kd->qk', query.astype(jnp.float32), keys.astype(jnp.float32)) * HEAD ** (-0.5)
    scores = jnp.where(segments[:, None] == segments[None, :], scores, -1e+30)
    highest = lax.optimization_barrier(jnp.max(scores, axis=1, keepdims=True))
    raised = jnp.exp(scores - highest)
    attn_weights = (raised / lax.optimization_barrier(jnp.sum(raised, axis=1, keepdims=True))).astype(jnp.bfloat16)
    return jnp.dot(attn_weights, values, preferred_element_type=jnp.float32).astype(jnp.bfloat16)

def reference(tokens, segment_ids, page_table, w_query, w_key, w_value, w_out, w_up, w_down, gain_first, shift_first, gain_second, shift_second):
    pages = tokens.reshape(NPAGES, PAGE, D)
    dealt = jnp.zeros_like(pages).at[page_table].set(pages).reshape(N_DP, TOK_DEV, D)
    dealt_ids = jnp.zeros((NPAGES, PAGE), jnp.int32).at[page_table].set(segment_ids.reshape(NPAGES, PAGE)).reshape(N_DP, TOK_DEV)
    group_heads = HEADS // N_MP
    group_width = D // N_MP
    group_units = FF // N_MP

    def device_layer(bundle):
        rows, segments = bundle
        query = jnp.dot(rows, w_query, preferred_element_type=jnp.float32).astype(jnp.bfloat16)
        keys = jnp.dot(rows, w_key, preferred_element_type=jnp.float32).astype(jnp.bfloat16)
        values = jnp.dot(rows, w_value, preferred_element_type=jnp.float32).astype(jnp.bfloat16)
        attended = jnp.zeros((TOK_DEV, D), jnp.float32)
        for group in range(N_MP):
            heads = []
            for head in range(group * group_heads, (group + 1) * group_heads):
                cols = slice(head * HEAD, (head + 1) * HEAD)
                heads.append(attend_head(query[:, cols], keys[:, cols], values[:, cols], segments))
            context = jnp.concatenate(heads, axis=1)
            term = jnp.dot(context, w_out[group * group_width:(group + 1) * group_width], preferred_element_type=jnp.float32).astype(jnp.bfloat16)
            attended = attended + lax.optimization_barrier(term).astype(jnp.float32)
        first = layer_norm(rows.astype(jnp.float32) + attended, gain_first, shift_first).astype(jnp.bfloat16)
        fed = jnp.zeros((TOK_DEV, D), jnp.float32)
        for group in range(N_MP):
            units = slice(group * group_units, (group + 1) * group_units)
            hidden = jax.nn.gelu(jnp.dot(first, w_up[:, units], preferred_element_type=jnp.float32), approximate=False).astype(jnp.bfloat16)
            term = jnp.dot(hidden, w_down[units], preferred_element_type=jnp.float32).astype(jnp.bfloat16)
            fed = fed + lax.optimization_barrier(term).astype(jnp.float32)
        second = layer_norm(first.astype(jnp.float32) + fed, gain_second, shift_second).astype(jnp.bfloat16)
        return (second, jnp.stack([keys, values], axis=1))
    second, cache = lax.map(device_layer, (dealt, dealt_ids))
    mixed = second.reshape(NPAGES, PAGE, D)[page_table].reshape(TOKENS, D)
    return (mixed, cache.reshape(TOKENS, 2, D))
```

```python
import jax
import jax.numpy as jnp
from jax import lax
from jax.sharding import PartitionSpec as P

HEAD = 64


def layer_norm(hidden_sum, gain, shift):
    center = hidden_sum - jnp.mean(hidden_sum, axis=-1, keepdims=True)
    spread = jnp.mean(center * center, axis=-1, keepdims=True)
    return center * lax.rsqrt(spread + 1e-05) * gain + shift


def attend_head(query, keys, values, segments, block_rows):
    blocks = query.shape[0] // block_rows
    query_blocks = query.reshape(blocks, block_rows, query.shape[1])
    segment_blocks = segments.reshape(blocks, block_rows)

    def per_block(bundle):
        rows, row_ids = bundle
        scores = jnp.einsum("qd,kd->qk", rows, keys, preferred_element_type=jnp.float32) * HEAD ** (
            -0.5
        )
        scores = jnp.where(row_ids[:, None] == segments[None, :], scores, -1e30)
        highest = jnp.max(scores, axis=1, keepdims=True)
        raised = jnp.exp(scores - highest)
        attn_weights = (raised / jnp.sum(raised, axis=1, keepdims=True)).astype(jnp.bfloat16)
        return jnp.dot(attn_weights, values, preferred_element_type=jnp.float32).astype(
            jnp.bfloat16
        )

    return lax.map(per_block, (query_blocks, segment_blocks)).reshape(
        query.shape[0], values.shape[1]
    )


def body(
    tokens,
    segment_ids,
    page_table,
    w_query,
    w_key,
    w_value,
    w_out,
    w_up,
    w_down,
    gain_first,
    shift_first,
    gain_second,
    shift_second,
):
    n_data = lax.axis_size("dp")
    n_model = lax.axis_size("mp")
    me_model = lax.axis_index("mp")
    pages_dev = page_table.shape[0]
    page = tokens.shape[0] // pages_dev
    width = tokens.shape[1]
    quarter = width // n_model
    sub = page // n_model
    slots_per = (pages_dev + n_data - 1) // n_data
    buffer_rows = n_data * slots_per

    head_cols = w_query.shape[1]
    unit_cols = w_up.shape[1]
    local = jnp.concatenate([w_query, w_key, w_value, w_up, w_out.T, w_down.T], axis=1)
    gathered = lax.all_gather(local, "dp", axis=0, tiled=True)
    at = 0
    full_query = gathered[:, at : at + head_cols]
    at += head_cols
    full_key = gathered[:, at : at + head_cols]
    at += head_cols
    full_value = gathered[:, at : at + head_cols]
    at += head_cols
    full_up = gathered[:, at : at + unit_cols]
    at += unit_cols
    out_t = gathered[:, at : at + w_out.shape[0]]
    at += w_out.shape[0]
    down_t = gathered[:, at : at + w_down.shape[0]]
    out_all_t = lax.all_gather(out_t, "mp", axis=1, tiled=True)

    target = page_table // pages_dev
    local_slot = page_table % pages_dev
    order = jnp.arange(pages_dev, dtype=jnp.int32)
    earlier = (target[:, None] == target[None, :]) & (order[:, None] < order[None, :])
    rank = jnp.sum(earlier.astype(jnp.int32), axis=0)
    position = target * slots_per + rank
    meta = jnp.concatenate(
        [segment_ids.reshape(pages_dev, page), local_slot[:, None]], axis=1
    )
    send_meta = (
        jnp.zeros((buffer_rows, page + 1), jnp.int32).at[:, page].set(-1).at[position].set(meta)
    )
    token_part = lax.dynamic_slice_in_dim(tokens, me_model * quarter, quarter, axis=1)
    send_pages = (
        jnp.zeros((buffer_rows, page, quarter), tokens.dtype)
        .at[position]
        .set(token_part.reshape(pages_dev, page, quarter))
    )
    got_pages = lax.all_to_all(send_pages, "dp", split_axis=0, concat_axis=0, tiled=True)
    got_meta = lax.all_to_all(send_meta, "dp", split_axis=0, concat_axis=0, tiled=True)
    got_ids = got_meta[:, :page]
    got_slots = got_meta[:, page]
    matches = got_slots[None, :] == order[:, None]
    source_row = jnp.sum(
        jnp.where(matches, jnp.arange(buffer_rows, dtype=jnp.int32)[None, :], 0), axis=1
    )
    dealt_part = got_pages[source_row]
    dealt = lax.all_gather(dealt_part, "mp", axis=2, tiled=True).reshape(pages_dev * page, width)
    dealt_ids = got_ids[source_row].reshape(pages_dev * page)

    query = jnp.dot(dealt, full_query, preferred_element_type=jnp.float32).astype(jnp.bfloat16)
    keys = jnp.dot(dealt, full_key, preferred_element_type=jnp.float32).astype(jnp.bfloat16)
    values = jnp.dot(dealt, full_value, preferred_element_type=jnp.float32).astype(jnp.bfloat16)
    suitable = [
        count for count in range(1, pages_dev + 1) if pages_dev % count == 0 and count * page >= 512
    ]
    block_rows = suitable[0] * page
    heads_here = query.shape[1] // HEAD
    contexts = []
    for head in range(heads_here):
        cols = slice(head * HEAD, (head + 1) * HEAD)
        contexts.append(
            attend_head(query[:, cols], keys[:, cols], values[:, cols], dealt_ids, block_rows)
        )
    context = jnp.concatenate(contexts, axis=1)

    context_rows = lax.all_to_all(
        context.reshape(pages_dev, n_model, sub, head_cols),
        "mp",
        split_axis=1,
        concat_axis=1,
        tiled=True,
    )
    attended = jnp.zeros((pages_dev, sub, width), jnp.float32)
    for group in range(n_model):
        term = jnp.einsum(
            "pic,oc->pio",
            context_rows[:, group],
            out_all_t[:, group * head_cols : (group + 1) * head_cols],
            preferred_element_type=jnp.float32,
        ).astype(jnp.bfloat16)
        attended = attended + term.astype(jnp.float32)
    dealt_mine = lax.dynamic_index_in_dim(
        dealt.reshape(pages_dev, n_model, sub, width), me_model, axis=1, keepdims=False
    )
    first_mine = layer_norm(
        dealt_mine.astype(jnp.float32) + attended, gain_first, shift_first
    ).astype(jnp.bfloat16)
    first = lax.all_gather(first_mine, "mp", axis=1).reshape(pages_dev * page, width)

    hidden = jax.nn.gelu(
        jnp.dot(first, full_up, preferred_element_type=jnp.float32), approximate=False
    ).astype(jnp.bfloat16)
    fed_term = jnp.einsum(
        "tu,ou->to", hidden, down_t, preferred_element_type=jnp.float32
    ).astype(jnp.bfloat16)
    fed = lax.psum_scatter(
        fed_term.reshape(pages_dev, n_model, sub, width), "mp", scatter_dimension=1, tiled=True
    ).reshape(pages_dev, sub, width)
    second_mine = layer_norm(
        first_mine.astype(jnp.float32) + fed.astype(jnp.float32), gain_second, shift_second
    ).astype(jnp.bfloat16)

    valid = got_slots >= 0
    outgoing = jnp.where(
        valid[:, None, None],
        second_mine[jnp.clip(got_slots, 0, pages_dev - 1)],
        jnp.zeros((), second_mine.dtype),
    )
    returned = lax.all_to_all(outgoing, "dp", split_axis=0, concat_axis=0, tiled=True)
    mixed_mine = returned[position]
    mixed = lax.all_gather(mixed_mine, "mp", axis=1).reshape(pages_dev * page, width)
    kv_cache = jnp.stack([keys, values], axis=1)
    return (mixed, kv_cache)


def solution(mesh):
    return jax.shard_map(
        body,
        mesh=mesh,
        in_specs=(
            P("dp", None),
            P("dp"),
            P("dp"),
            P("dp", "mp"),
            P("dp", "mp"),
            P("dp", "mp"),
            P("mp", "dp"),
            P("dp", "mp"),
            P("mp", "dp"),
            P(),
            P(),
            P(),
            P(),
        ),
        out_specs=(P("dp", None), P("dp", None, "mp")),
        check_vma=False,
    )
```

```python
import jax
import jax.numpy as jnp
from jax import lax
from jax.sharding import PartitionSpec as P

HEAD = 64


def layer_norm(hidden_sum, gain, shift):
    center = hidden_sum - jnp.mean(hidden_sum, axis=-1, keepdims=True)
    spread = jnp.mean(center * center, axis=-1, keepdims=True)
    return center * lax.rsqrt(spread + 1e-05) * gain + shift


def attend_head(query, keys, values, segments, block_rows):
    blocks = query.shape[0] // block_rows
    query_blocks = query.reshape(blocks, block_rows, query.shape[1])
    segment_blocks = segments.reshape(blocks, block_rows)

    def per_block(bundle):
        rows, row_ids = bundle
        scores = jnp.einsum("qd,kd->qk", rows, keys, preferred_element_type=jnp.float32) * HEAD ** (
            -0.5
        )
        scores = jnp.where(row_ids[:, None] == segments[None, :], scores, -1e30)
        highest = jnp.max(scores, axis=1, keepdims=True)
        raised = jnp.exp(scores - highest)
        attn_weights = (raised / jnp.sum(raised, axis=1, keepdims=True)).astype(jnp.bfloat16)
        return jnp.dot(attn_weights, values, preferred_element_type=jnp.float32).astype(
            jnp.bfloat16
        )

    return lax.map(per_block, (query_blocks, segment_blocks)).reshape(
        query.shape[0], values.shape[1]
    )


def body(
    tokens,
    segment_ids,
    page_table,
    w_query,
    w_key,
    w_value,
    w_out,
    w_up,
    w_down,
    gain_first,
    shift_first,
    gain_second,
    shift_second,
):
    n_data = lax.axis_size("dp")
    n_model = lax.axis_size("mp")
    me_model = lax.axis_index("mp")
    pages_dev = page_table.shape[0]
    page = tokens.shape[0] // pages_dev
    width = tokens.shape[1]
    quarter = width // n_model
    sub = page // n_model
    slots_per = (pages_dev + n_data - 1) // n_data
    buffer_rows = n_data * slots_per

    head_cols = w_query.shape[1]
    in_part = w_out.shape[0]
    unit_part = w_up.shape[1]
    small = jnp.concatenate([w_out.T, w_up, w_down.T], axis=1)
    small_all = lax.all_gather(small, "mp", axis=1)
    rows_dp = small.shape[0]
    out_rows = small_all[:, :, :in_part].reshape(rows_dp, n_model * in_part)
    up_rows = small_all[:, :, in_part : in_part + unit_part].reshape(rows_dp, n_model * unit_part)
    down_rows = small_all[:, :, in_part + unit_part :].reshape(rows_dp, n_model * unit_part)
    attn_local = jnp.concatenate([w_query, w_key, w_value, out_rows], axis=1)
    attn_gathered = lax.all_gather(attn_local, "dp", axis=0, tiled=True)
    full_query = attn_gathered[:, :head_cols]
    full_key = attn_gathered[:, head_cols : 2 * head_cols]
    full_value = attn_gathered[:, 2 * head_cols : 3 * head_cols]
    out_all_t = attn_gathered[:, 3 * head_cols :]
    ffn_local = jnp.concatenate([up_rows, down_rows], axis=1)

    target = page_table // pages_dev
    local_slot = page_table % pages_dev
    order = jnp.arange(pages_dev, dtype=jnp.int32)
    earlier = (target[:, None] == target[None, :]) & (order[:, None] < order[None, :])
    rank = jnp.sum(earlier.astype(jnp.int32), axis=0)
    position = target * slots_per + rank
    meta = jnp.concatenate(
        [segment_ids.reshape(pages_dev, page), local_slot[:, None]], axis=1
    )
    send_meta = (
        jnp.zeros((buffer_rows, page + 1), jnp.int32).at[:, page].set(-1).at[position].set(meta)
    )
    token_part = lax.dynamic_slice_in_dim(tokens, me_model * quarter, quarter, axis=1)
    send_pages = (
        jnp.zeros((buffer_rows, page, quarter), tokens.dtype)
        .at[position]
        .set(token_part.reshape(pages_dev, page, quarter))
    )
    got_pages = lax.all_to_all(send_pages, "dp", split_axis=0, concat_axis=0, tiled=True)
    got_meta = lax.all_to_all(send_meta, "dp", split_axis=0, concat_axis=0, tiled=True)
    got_ids = got_meta[:, :page]
    got_slots = got_meta[:, page]
    matches = got_slots[None, :] == order[:, None]
    source_row = jnp.sum(
        jnp.where(matches, jnp.arange(buffer_rows, dtype=jnp.int32)[None, :], 0), axis=1
    )
    dealt_part = got_pages[source_row]
    dealt_part, attn_gathered = lax.optimization_barrier((dealt_part, attn_gathered))
    dealt = lax.all_gather(dealt_part, "mp", axis=2, tiled=True).reshape(pages_dev * page, width)
    dealt_ids = got_ids[source_row].reshape(pages_dev * page)
    ffn_local, dealt = lax.optimization_barrier((ffn_local, dealt))
    ffn_gathered = lax.all_gather(ffn_local, "dp", axis=0, tiled=True)
    units = n_model * unit_part
    full_up = ffn_gathered[:, :units]
    down_t = ffn_gathered[:, units:]

    query = jnp.dot(dealt, full_query, preferred_element_type=jnp.float32).astype(jnp.bfloat16)
    keys = jnp.dot(dealt, full_key, preferred_element_type=jnp.float32).astype(jnp.bfloat16)
    values = jnp.dot(dealt, full_value, preferred_element_type=jnp.float32).astype(jnp.bfloat16)
    suitable = [
        count for count in range(1, pages_dev + 1) if pages_dev % count == 0 and count * page >= 512
    ]
    block_rows = suitable[0] * page
    heads_here = query.shape[1] // HEAD
    contexts = []
    for head in range(heads_here):
        cols = slice(head * HEAD, (head + 1) * HEAD)
        contexts.append(
            attend_head(query[:, cols], keys[:, cols], values[:, cols], dealt_ids, block_rows)
        )
    context = jnp.concatenate(contexts, axis=1)

    context_rows = lax.all_to_all(
        context.reshape(pages_dev, n_model, sub, head_cols),
        "mp",
        split_axis=1,
        concat_axis=1,
        tiled=True,
    )
    attended = jnp.zeros((pages_dev, sub, width), jnp.float32)
    for group in range(n_model):
        term = jnp.einsum(
            "pic,oc->pio",
            context_rows[:, group],
            out_all_t[:, group * head_cols : (group + 1) * head_cols],
            preferred_element_type=jnp.float32,
        ).astype(jnp.bfloat16)
        attended = attended + term.astype(jnp.float32)
    dealt_mine = lax.dynamic_index_in_dim(
        dealt.reshape(pages_dev, n_model, sub, width), me_model, axis=1, keepdims=False
    )
    first_mine = layer_norm(
        dealt_mine.astype(jnp.float32) + attended, gain_first, shift_first
    ).astype(jnp.bfloat16)
    hidden = jax.nn.gelu(
        jnp.einsum("pid,du->piu", first_mine, full_up, preferred_element_type=jnp.float32),
        approximate=False,
    ).astype(jnp.bfloat16)
    fed = jnp.zeros((pages_dev, sub, width), jnp.float32)
    for group in range(n_model):
        term = jnp.einsum(
            "piu,ou->pio",
            hidden[:, :, group * unit_part : (group + 1) * unit_part],
            down_t[:, group * unit_part : (group + 1) * unit_part],
            preferred_element_type=jnp.float32,
        ).astype(jnp.bfloat16)
        fed = fed + term.astype(jnp.float32)
    second_mine = layer_norm(first_mine.astype(jnp.float32) + fed, gain_second, shift_second).astype(
        jnp.bfloat16
    )

    valid = got_slots >= 0
    outgoing = jnp.where(
        valid[:, None, None],
        second_mine[jnp.clip(got_slots, 0, pages_dev - 1)],
        jnp.zeros((), second_mine.dtype),
    )
    returned = lax.all_to_all(outgoing, "dp", split_axis=0, concat_axis=0, tiled=True)
    mixed_mine = returned[position]
    mixed = lax.all_gather(mixed_mine, "mp", axis=1).reshape(pages_dev * page, width)
    kv_cache = jnp.stack([keys, values], axis=1)
    return (mixed, kv_cache)


def solution(mesh):
    return jax.shard_map(
        body,
        mesh=mesh,
        in_specs=(
            P("dp", None),
            P("dp"),
            P("dp"),
            P("dp", "mp"),
            P("dp", "mp"),
            P("dp", "mp"),
            P("mp", "dp"),
            P("dp", "mp"),
            P("mp", "dp"),
            P(),
            P(),
            P(),
            P(),
        ),
        out_specs=(P("dp", None), P("dp", None, "mp")),
        check_vma=False,
    )
```

```python
import jax
import jax.numpy as jnp
from jax import lax
from jax.sharding import PartitionSpec as P

HEAD = 64


def layer_norm(hidden_sum, gain, shift):
    center = hidden_sum - jnp.mean(hidden_sum, axis=-1, keepdims=True)
    spread = jnp.mean(center * center, axis=-1, keepdims=True)
    return center * lax.rsqrt(spread + 1e-05) * gain + shift


def attend_head(query, keys, values, segments, block_rows):
    blocks = query.shape[0] // block_rows
    query_blocks = query.reshape(blocks, block_rows, query.shape[1])
    segment_blocks = segments.reshape(blocks, block_rows)

    def per_block(bundle):
        rows, row_ids = bundle
        scores = jnp.einsum("qd,kd->qk", rows, keys, preferred_element_type=jnp.float32) * HEAD ** (
            -0.5
        )
        scores = jnp.where(row_ids[:, None] == segments[None, :], scores, -1e30)
        highest = jnp.max(scores, axis=1, keepdims=True)
        raised = jnp.exp(scores - highest)
        attn_weights = (raised / jnp.sum(raised, axis=1, keepdims=True)).astype(jnp.bfloat16)
        return jnp.dot(attn_weights, values, preferred_element_type=jnp.float32).astype(
            jnp.bfloat16
        )

    return lax.map(per_block, (query_blocks, segment_blocks)).reshape(
        query.shape[0], values.shape[1]
    )


def body(
    tokens,
    segment_ids,
    page_table,
    w_query,
    w_key,
    w_value,
    w_out,
    w_up,
    w_down,
    gain_first,
    shift_first,
    gain_second,
    shift_second,
):
    n_data = lax.axis_size("dp")
    n_model = lax.axis_size("mp")
    me_model = lax.axis_index("mp")
    pages_dev = page_table.shape[0]
    page = tokens.shape[0] // pages_dev
    width = tokens.shape[1]
    quarter = width // n_model
    sub = page // n_model
    slots_per = (pages_dev + n_data - 1) // n_data
    buffer_rows = n_data * slots_per

    head_cols = w_query.shape[1]
    in_part = w_out.shape[0]
    unit_part = w_up.shape[1]
    attn_local = jnp.concatenate([w_query, w_key, w_value], axis=1)
    attn_gathered = lax.all_gather(attn_local, "dp", axis=0, tiled=True)
    full_query = attn_gathered[:, :head_cols]
    full_key = attn_gathered[:, head_cols : 2 * head_cols]
    full_value = attn_gathered[:, 2 * head_cols : 3 * head_cols]
    small = jnp.concatenate([w_out.T, w_up, w_down.T], axis=1)

    target = page_table // pages_dev
    local_slot = page_table % pages_dev
    order = jnp.arange(pages_dev, dtype=jnp.int32)
    earlier = (target[:, None] == target[None, :]) & (order[:, None] < order[None, :])
    rank = jnp.sum(earlier.astype(jnp.int32), axis=0)
    position = target * slots_per + rank
    meta = jnp.zeros((pages_dev, 1, quarter), tokens.dtype)
    meta = meta.at[:, 0, :page].set(segment_ids.reshape(pages_dev, page).astype(tokens.dtype))
    meta = meta.at[:, 0, page].set(local_slot.astype(tokens.dtype))
    token_part = lax.dynamic_slice_in_dim(tokens, me_model * quarter, quarter, axis=1)
    with_meta = jnp.concatenate([token_part.reshape(pages_dev, page, quarter), meta], axis=1)
    send_pages = (
        jnp.zeros((buffer_rows, page + 1, quarter), tokens.dtype)
        .at[:, page, page]
        .set(-1)
        .at[position]
        .set(with_meta)
    )
    small, send_pages = lax.optimization_barrier((small, send_pages))
    got_all = lax.all_to_all(send_pages, "dp", split_axis=0, concat_axis=0, tiled=True)
    got_pages = got_all[:, :page]
    got_ids = got_all[:, page, :page].astype(jnp.int32)
    got_slots = got_all[:, page, page].astype(jnp.int32)
    matches = got_slots[None, :] == order[:, None]
    source_row = jnp.sum(
        jnp.where(matches, jnp.arange(buffer_rows, dtype=jnp.int32)[None, :], 0), axis=1
    )
    small_all = lax.all_gather(small, "mp", axis=1)
    rows_dp = small.shape[0]
    out_rows = small_all[:, :, :in_part].reshape(rows_dp, n_model * in_part)
    up_rows = small_all[:, :, in_part : in_part + unit_part].reshape(rows_dp, n_model * unit_part)
    down_rows = small_all[:, :, in_part + unit_part :].reshape(rows_dp, n_model * unit_part)
    ffn_local = jnp.concatenate([out_rows, up_rows, down_rows], axis=1)
    dealt_part = got_pages[source_row]
    dealt_part, attn_gathered = lax.optimization_barrier((dealt_part, attn_gathered))
    dealt = lax.all_gather(dealt_part, "mp", axis=2, tiled=True).reshape(pages_dev * page, width)
    dealt_ids = got_ids[source_row].reshape(pages_dev * page)
    ffn_local, dealt = lax.optimization_barrier((ffn_local, dealt))
    ffn_gathered = lax.all_gather(ffn_local, "dp", axis=0, tiled=True)
    units = n_model * unit_part
    in_all = n_model * in_part
    out_all_t = ffn_gathered[:, :in_all]
    full_up = ffn_gathered[:, in_all : in_all + units]
    down_t = ffn_gathered[:, in_all + units :]

    query = jnp.dot(dealt, full_query, preferred_element_type=jnp.float32).astype(jnp.bfloat16)
    keys = jnp.dot(dealt, full_key, preferred_element_type=jnp.float32).astype(jnp.bfloat16)
    values = jnp.dot(dealt, full_value, preferred_element_type=jnp.float32).astype(jnp.bfloat16)
    suitable = [
        count for count in range(1, pages_dev + 1) if pages_dev % count == 0 and count * page >= 512
    ]
    block_rows = suitable[0] * page
    heads_here = query.shape[1] // HEAD
    contexts = []
    for head in range(heads_here):
        cols = slice(head * HEAD, (head + 1) * HEAD)
        contexts.append(
            attend_head(query[:, cols], keys[:, cols], values[:, cols], dealt_ids, block_rows)
        )
    context = jnp.concatenate(contexts, axis=1)

    context_rows = lax.all_to_all(
        context.reshape(pages_dev, n_model, sub, head_cols),
        "mp",
        split_axis=1,
        concat_axis=1,
        tiled=True,
    )
    attended = jnp.zeros((pages_dev, sub, width), jnp.float32)
    for group in range(n_model):
        term = jnp.einsum(
            "pic,oc->pio",
            context_rows[:, group],
            out_all_t[:, group * head_cols : (group + 1) * head_cols],
            preferred_element_type=jnp.float32,
        ).astype(jnp.bfloat16)
        attended = attended + term.astype(jnp.float32)
    dealt_mine = lax.dynamic_index_in_dim(
        dealt.reshape(pages_dev, n_model, sub, width), me_model, axis=1, keepdims=False
    )
    first_mine = layer_norm(
        dealt_mine.astype(jnp.float32) + attended, gain_first, shift_first
    ).astype(jnp.bfloat16)
    hidden = jax.nn.gelu(
        jnp.einsum("pid,du->piu", first_mine, full_up, preferred_element_type=jnp.float32),
        approximate=False,
    ).astype(jnp.bfloat16)
    fed = jnp.zeros((pages_dev, sub, width), jnp.float32)
    for group in range(n_model):
        term = jnp.einsum(
            "piu,ou->pio",
            hidden[:, :, group * unit_part : (group + 1) * unit_part],
            down_t[:, group * unit_part : (group + 1) * unit_part],
            preferred_element_type=jnp.float32,
        ).astype(jnp.bfloat16)
        fed = fed + term.astype(jnp.float32)
    second_mine = layer_norm(first_mine.astype(jnp.float32) + fed, gain_second, shift_second).astype(
        jnp.bfloat16
    )

    valid = got_slots >= 0
    outgoing = jnp.where(
        valid[:, None, None],
        second_mine[jnp.clip(got_slots, 0, pages_dev - 1)],
        jnp.zeros((), second_mine.dtype),
    )
    returned = lax.all_to_all(outgoing, "dp", split_axis=0, concat_axis=0, tiled=True)
    mixed_mine = returned[position]
    mixed = lax.all_gather(mixed_mine, "mp", axis=1).reshape(pages_dev * page, width)
    kv_cache = jnp.stack([keys, values], axis=1)
    return (mixed, kv_cache)


def solution(mesh):
    return jax.shard_map(
        body,
        mesh=mesh,
        in_specs=(
            P("dp", None),
            P("dp"),
            P("dp"),
            P("dp", "mp"),
            P("dp", "mp"),
            P("dp", "mp"),
            P("mp", "dp"),
            P("dp", "mp"),
            P("mp", "dp"),
            P(),
            P(),
            P(),
            P(),
        ),
        out_specs=(P("dp", None), P("dp", None, "mp")),
        check_vma=False,
    )
```

```python
import jax
import jax.numpy as jnp
from jax import lax
from jax.experimental import pallas as pl
from jax.sharding import PartitionSpec as P

HEAD = 64


def layer_norm(hidden_sum, gain, shift):
    center = hidden_sum - jnp.mean(hidden_sum, axis=-1, keepdims=True)
    spread = jnp.mean(center * center, axis=-1, keepdims=True)
    return center * lax.rsqrt(spread + 1e-05) * gain + shift


def _attn_kernel(q_ref, k_ref, v_ref, qid_ref, kid_ref, o_ref):
    scores = lax.dot_general(
        q_ref[0], k_ref[0], (((1,), (1,)), ((), ())), preferred_element_type=jnp.float32
    ) * (HEAD ** -0.5)
    scores = jnp.where(qid_ref[...] == kid_ref[...], scores, -1e30)
    highest = jnp.max(scores, axis=1, keepdims=True)
    raised = jnp.exp(scores - highest)
    weights = (raised / jnp.sum(raised, axis=1, keepdims=True)).astype(jnp.bfloat16)
    o_ref[0] = jnp.dot(weights, v_ref[0], preferred_element_type=jnp.float32).astype(o_ref.dtype)


def attention(q, k, v, ids, block_q=256):
    heads, rows, dim = q.shape
    qid = ids.reshape(rows, 1)
    kid = ids.reshape(1, rows)
    return pl.pallas_call(
        _attn_kernel,
        out_shape=jax.ShapeDtypeStruct((heads, rows, dim), jnp.bfloat16),
        grid=(heads, rows // block_q),
        in_specs=[
            pl.BlockSpec((1, block_q, dim), lambda h, i: (h, i, 0)),
            pl.BlockSpec((1, rows, dim), lambda h, i: (h, 0, 0)),
            pl.BlockSpec((1, rows, dim), lambda h, i: (h, 0, 0)),
            pl.BlockSpec((block_q, 1), lambda h, i: (i, 0)),
            pl.BlockSpec((1, rows), lambda h, i: (0, 0)),
        ],
        out_specs=pl.BlockSpec((1, block_q, dim), lambda h, i: (h, i, 0)),
        cost_estimate=pl.CostEstimate(
            flops=4 * heads * rows * rows * dim,
            transcendentals=heads * rows * rows,
            bytes_accessed=4 * heads * rows * dim * 2,
        ),
    )(q, k, v, qid, kid)


def body(
    tokens,
    segment_ids,
    page_table,
    w_query,
    w_key,
    w_value,
    w_out,
    w_up,
    w_down,
    gain_first,
    shift_first,
    gain_second,
    shift_second,
):
    n_data = lax.axis_size("dp")
    n_model = lax.axis_size("mp")
    me_model = lax.axis_index("mp")
    pages_dev = page_table.shape[0]
    page = tokens.shape[0] // pages_dev
    width = tokens.shape[1]
    quarter = width // n_model
    sub = page // n_model
    slots_per = (pages_dev + n_data - 1) // n_data
    buffer_rows = n_data * slots_per

    head_cols = w_query.shape[1]
    in_part = w_out.shape[0]
    unit_part = w_up.shape[1]
    attn_local = jnp.concatenate([w_query, w_key, w_value], axis=1)
    attn_gathered = lax.all_gather(attn_local, "dp", axis=0, tiled=True)
    full_query = attn_gathered[:, :head_cols]
    full_key = attn_gathered[:, head_cols : 2 * head_cols]
    full_value = attn_gathered[:, 2 * head_cols : 3 * head_cols]
    small = jnp.concatenate([w_out.T, w_up, w_down.T], axis=1)

    target = page_table // pages_dev
    local_slot = page_table % pages_dev
    order = jnp.arange(pages_dev, dtype=jnp.int32)
    earlier = (target[:, None] == target[None, :]) & (order[:, None] < order[None, :])
    rank = jnp.sum(earlier.astype(jnp.int32), axis=0)
    position = target * slots_per + rank
    meta = jnp.zeros((pages_dev, 1, quarter), tokens.dtype)
    meta = meta.at[:, 0, :page].set(segment_ids.reshape(pages_dev, page).astype(tokens.dtype))
    meta = meta.at[:, 0, page].set(local_slot.astype(tokens.dtype))
    token_part = lax.dynamic_slice_in_dim(tokens, me_model * quarter, quarter, axis=1)
    with_meta = jnp.concatenate([token_part.reshape(pages_dev, page, quarter), meta], axis=1)
    send_pages = (
        jnp.zeros((buffer_rows, page + 1, quarter), tokens.dtype)
        .at[:, page, page]
        .set(-1)
        .at[position]
        .set(with_meta)
    )
    small, send_pages = lax.optimization_barrier((small, send_pages))
    got_all = lax.all_to_all(send_pages, "dp", split_axis=0, concat_axis=0, tiled=True)
    got_pages = got_all[:, :page]
    got_ids = got_all[:, page, :page].astype(jnp.int32)
    got_slots = got_all[:, page, page].astype(jnp.int32)
    matches = got_slots[None, :] == order[:, None]
    source_row = jnp.sum(
        jnp.where(matches, jnp.arange(buffer_rows, dtype=jnp.int32)[None, :], 0), axis=1
    )
    small_all = lax.all_gather(small, "mp", axis=1)
    rows_dp = small.shape[0]
    out_rows = small_all[:, :, :in_part].reshape(rows_dp, n_model * in_part)
    up_rows = small_all[:, :, in_part : in_part + unit_part].reshape(rows_dp, n_model * unit_part)
    down_rows = small_all[:, :, in_part + unit_part :].reshape(rows_dp, n_model * unit_part)
    ffn_local = jnp.concatenate([out_rows, up_rows, down_rows], axis=1)
    dealt_part = got_pages[source_row]
    dealt_part, attn_gathered = lax.optimization_barrier((dealt_part, attn_gathered))
    dealt = lax.all_gather(dealt_part, "mp", axis=2, tiled=True).reshape(pages_dev * page, width)
    dealt_ids = got_ids[source_row].reshape(pages_dev * page)
    ffn_local, dealt = lax.optimization_barrier((ffn_local, dealt))
    ffn_gathered = lax.all_gather(ffn_local, "dp", axis=0, tiled=True)
    units = n_model * unit_part
    in_all = n_model * in_part
    out_all_t = ffn_gathered[:, :in_all]
    full_up = ffn_gathered[:, in_all : in_all + units]
    down_t = ffn_gathered[:, in_all + units :]

    query = jnp.dot(dealt, full_query, preferred_element_type=jnp.float32).astype(jnp.bfloat16)
    keys = jnp.dot(dealt, full_key, preferred_element_type=jnp.float32).astype(jnp.bfloat16)
    values = jnp.dot(dealt, full_value, preferred_element_type=jnp.float32).astype(jnp.bfloat16)
    heads_here = query.shape[1] // HEAD
    rows = query.shape[0]

    def by_head(x):
        return x.reshape(rows, heads_here, HEAD).transpose(1, 0, 2)

    context = (
        attention(by_head(query), by_head(keys), by_head(values), dealt_ids)
        .transpose(1, 0, 2)
        .reshape(rows, heads_here * HEAD)
    )

    context_rows = lax.all_to_all(
        context.reshape(pages_dev, n_model, sub, head_cols),
        "mp",
        split_axis=1,
        concat_axis=1,
        tiled=True,
    )
    attended = jnp.zeros((pages_dev, sub, width), jnp.float32)
    for group in range(n_model):
        term = jnp.einsum(
            "pic,oc->pio",
            context_rows[:, group],
            out_all_t[:, group * head_cols : (group + 1) * head_cols],
            preferred_element_type=jnp.float32,
        ).astype(jnp.bfloat16)
        attended = attended + term.astype(jnp.float32)
    dealt_mine = lax.dynamic_index_in_dim(
        dealt.reshape(pages_dev, n_model, sub, width), me_model, axis=1, keepdims=False
    )
    first_mine = layer_norm(
        dealt_mine.astype(jnp.float32) + attended, gain_first, shift_first
    ).astype(jnp.bfloat16)
    hidden = jax.nn.gelu(
        jnp.einsum("pid,du->piu", first_mine, full_up, preferred_element_type=jnp.float32),
        approximate=False,
    ).astype(jnp.bfloat16)
    fed = jnp.zeros((pages_dev, sub, width), jnp.float32)
    for group in range(n_model):
        term = jnp.einsum(
            "piu,ou->pio",
            hidden[:, :, group * unit_part : (group + 1) * unit_part],
            down_t[:, group * unit_part : (group + 1) * unit_part],
            preferred_element_type=jnp.float32,
        ).astype(jnp.bfloat16)
        fed = fed + term.astype(jnp.float32)
    second_mine = layer_norm(first_mine.astype(jnp.float32) + fed, gain_second, shift_second).astype(
        jnp.bfloat16
    )

    valid = got_slots >= 0
    outgoing = jnp.where(
        valid[:, None, None],
        second_mine[jnp.clip(got_slots, 0, pages_dev - 1)],
        jnp.zeros((), second_mine.dtype),
    )
    returned = lax.all_to_all(outgoing, "dp", split_axis=0, concat_axis=0, tiled=True)
    mixed_mine = returned[position]
    mixed = lax.all_gather(mixed_mine, "mp", axis=1).reshape(pages_dev * page, width)
    kv_cache = jnp.stack([keys, values], axis=1)
    return (mixed, kv_cache)


def solution(mesh):
    return jax.shard_map(
        body,
        mesh=mesh,
        in_specs=(
            P("dp", None),
            P("dp"),
            P("dp"),
            P("dp", "mp"),
            P("dp", "mp"),
            P("dp", "mp"),
            P("mp", "dp"),
            P("dp", "mp"),
            P("mp", "dp"),
            P(),
            P(),
            P(),
            P(),
        ),
        out_specs=(P("dp", None), P("dp", None, "mp")),
        check_vma=False,
    )
```

```python
import jax
import jax.numpy as jnp
from jax import lax
from jax.experimental import pallas as pl
from jax.experimental.pallas import tpu as pltpu
from jax.sharding import PartitionSpec as P

HEAD = 64


def layer_norm(hidden_sum, gain, shift):
    center = hidden_sum - jnp.mean(hidden_sum, axis=-1, keepdims=True)
    spread = jnp.mean(center * center, axis=-1, keepdims=True)
    return center * lax.rsqrt(spread + 1e-05) * gain + shift


KEY_CHUNK = 256


def _attn_kernel(lo_ref, hi_ref, q_ref, k_ref, v_ref, qid_ref, kid_ref, o_ref, s_ref):
    block = pl.program_id(0)
    lo = lo_ref[block]
    hi = hi_ref[block]
    rows = q_ref.shape[1]
    qid = qid_ref[...]
    for head in range(q_ref.shape[0]):
        q = q_ref[head]

        def score_step(c, highest):
            at = pl.multiple_of(c * KEY_CHUNK, KEY_CHUNK)
            keys = k_ref[head, pl.ds(at, KEY_CHUNK), :]
            scores = lax.dot_general(
                q, keys, (((1,), (1,)), ((), ())), preferred_element_type=jnp.float32
            ) * (HEAD ** -0.5)
            scores = jnp.where(qid == kid_ref[:, pl.ds(at, KEY_CHUNK)], scores, -1e30)
            s_ref[:, pl.ds(at, KEY_CHUNK)] = scores
            return jnp.maximum(highest, jnp.max(scores, axis=1, keepdims=True))

        highest = lax.fori_loop(
            lo, hi, score_step, jnp.full((rows, 1), -jnp.inf, jnp.float32)
        )

        def exp_step(c, total):
            at = pl.multiple_of(c * KEY_CHUNK, KEY_CHUNK)
            raised = jnp.exp(s_ref[:, pl.ds(at, KEY_CHUNK)] - highest)
            s_ref[:, pl.ds(at, KEY_CHUNK)] = raised
            return total + jnp.sum(raised, axis=1, keepdims=True)

        total = lax.fori_loop(lo, hi, exp_step, jnp.zeros((rows, 1), jnp.float32))

        def value_step(c, acc):
            at = pl.multiple_of(c * KEY_CHUNK, KEY_CHUNK)
            weights = (s_ref[:, pl.ds(at, KEY_CHUNK)] / total).astype(jnp.bfloat16)
            return acc + jnp.dot(
                weights, v_ref[head, pl.ds(at, KEY_CHUNK), :], preferred_element_type=jnp.float32
            )

        acc = lax.fori_loop(lo, hi, value_step, jnp.zeros((rows, HEAD), jnp.float32))
        o_ref[:, head * HEAD : (head + 1) * HEAD] = acc.astype(o_ref.dtype)


def key_ranges(ids, block_q):
    rows = ids.shape[0]
    index = jnp.arange(rows, dtype=jnp.int32)
    new_run = jnp.concatenate([jnp.ones((1,), bool), ids[1:] != ids[:-1]])
    run_start = lax.cummax(jnp.where(new_run, index, 0))
    run_last = jnp.concatenate([ids[1:] != ids[:-1], jnp.ones((1,), bool)])
    run_end = lax.cummin(jnp.where(run_last, index + 1, rows), reverse=True)
    lo = run_start[::block_q] // KEY_CHUNK
    hi = (run_end[block_q - 1 :: block_q] + KEY_CHUNK - 1) // KEY_CHUNK
    return lo.astype(jnp.int32), hi.astype(jnp.int32)


def attention(q, k, v, ids, block_q=256):
    heads, rows, dim = q.shape
    lo, hi = key_ranges(ids, block_q)
    qid = ids.reshape(rows, 1)
    kid = ids.reshape(1, rows)
    return pl.pallas_call(
        _attn_kernel,
        out_shape=jax.ShapeDtypeStruct((rows, heads * dim), jnp.bfloat16),
        grid_spec=pltpu.PrefetchScalarGridSpec(
            num_scalar_prefetch=2,
            grid=(rows // block_q,),
            in_specs=[
                pl.BlockSpec((heads, block_q, dim), lambda i, lo, hi: (0, i, 0)),
                pl.BlockSpec((heads, rows, dim), lambda i, lo, hi: (0, 0, 0)),
                pl.BlockSpec((heads, rows, dim), lambda i, lo, hi: (0, 0, 0)),
                pl.BlockSpec((block_q, 1), lambda i, lo, hi: (i, 0)),
                pl.BlockSpec((1, rows), lambda i, lo, hi: (0, 0)),
            ],
            out_specs=pl.BlockSpec((block_q, heads * dim), lambda i, lo, hi: (i, 0)),
            scratch_shapes=[pltpu.VMEM((block_q, rows), jnp.float32)],
        ),
        cost_estimate=pl.CostEstimate(
            flops=2 * heads * rows * rows * dim,
            transcendentals=heads * rows * rows // 2,
            bytes_accessed=4 * heads * rows * dim * 2,
        ),
    )(lo, hi, q, k, v, qid, kid)


def body(
    tokens,
    segment_ids,
    page_table,
    w_query,
    w_key,
    w_value,
    w_out,
    w_up,
    w_down,
    gain_first,
    shift_first,
    gain_second,
    shift_second,
):
    n_data = lax.axis_size("dp")
    n_model = lax.axis_size("mp")
    me_model = lax.axis_index("mp")
    pages_dev = page_table.shape[0]
    page = tokens.shape[0] // pages_dev
    width = tokens.shape[1]
    quarter = width // n_model
    sub = page // n_model
    slots_per = (pages_dev + n_data - 1) // n_data
    buffer_rows = n_data * slots_per

    head_cols = w_query.shape[1]
    in_part = w_out.shape[0]
    unit_part = w_up.shape[1]
    attn_local = jnp.concatenate([w_query, w_key, w_value], axis=1)
    attn_gathered = lax.all_gather(attn_local, "dp", axis=0, tiled=True)
    full_query = attn_gathered[:, :head_cols]
    full_key = attn_gathered[:, head_cols : 2 * head_cols]
    full_value = attn_gathered[:, 2 * head_cols : 3 * head_cols]
    small = jnp.concatenate([w_out.T, w_up, w_down.T], axis=1)

    target = page_table // pages_dev
    local_slot = page_table % pages_dev
    order = jnp.arange(pages_dev, dtype=jnp.int32)
    earlier = (target[:, None] == target[None, :]) & (order[:, None] < order[None, :])
    rank = jnp.sum(earlier.astype(jnp.int32), axis=0)
    position = target * slots_per + rank
    meta = jnp.zeros((pages_dev, 1, quarter), tokens.dtype)
    meta = meta.at[:, 0, :page].set(segment_ids.reshape(pages_dev, page).astype(tokens.dtype))
    meta = meta.at[:, 0, page].set(local_slot.astype(tokens.dtype))
    token_part = lax.dynamic_slice_in_dim(tokens, me_model * quarter, quarter, axis=1)
    with_meta = jnp.concatenate([token_part.reshape(pages_dev, page, quarter), meta], axis=1)
    send_pages = (
        jnp.zeros((buffer_rows, page + 1, quarter), tokens.dtype)
        .at[:, page, page]
        .set(-1)
        .at[position]
        .set(with_meta)
    )
    small, send_pages = lax.optimization_barrier((small, send_pages))
    got_all = lax.all_to_all(send_pages, "dp", split_axis=0, concat_axis=0, tiled=True)
    got_pages = got_all[:, :page]
    got_ids = got_all[:, page, :page].astype(jnp.int32)
    got_slots = got_all[:, page, page].astype(jnp.int32)
    matches = got_slots[None, :] == order[:, None]
    source_row = jnp.sum(
        jnp.where(matches, jnp.arange(buffer_rows, dtype=jnp.int32)[None, :], 0), axis=1
    )
    small_all = lax.all_gather(small, "mp", axis=1)
    rows_dp = small.shape[0]
    out_rows = small_all[:, :, :in_part].reshape(rows_dp, n_model * in_part)
    up_rows = small_all[:, :, in_part : in_part + unit_part].reshape(rows_dp, n_model * unit_part)
    down_rows = small_all[:, :, in_part + unit_part :].reshape(rows_dp, n_model * unit_part)
    ffn_local = jnp.concatenate([out_rows, up_rows, down_rows], axis=1)
    dealt_part = got_pages[source_row]
    dealt_part, attn_gathered = lax.optimization_barrier((dealt_part, attn_gathered))
    dealt = lax.all_gather(dealt_part, "mp", axis=2, tiled=True).reshape(pages_dev * page, width)
    dealt_ids = got_ids[source_row].reshape(pages_dev * page)
    ffn_local, dealt = lax.optimization_barrier((ffn_local, dealt))
    ffn_gathered = lax.all_gather(ffn_local, "dp", axis=0, tiled=True)
    units = n_model * unit_part
    in_all = n_model * in_part
    out_all_t = ffn_gathered[:, :in_all]
    full_up = ffn_gathered[:, in_all : in_all + units]
    down_t = ffn_gathered[:, in_all + units :]

    query = jnp.dot(dealt, full_query, preferred_element_type=jnp.float32).astype(jnp.bfloat16)
    keys = jnp.dot(dealt, full_key, preferred_element_type=jnp.float32).astype(jnp.bfloat16)
    values = jnp.dot(dealt, full_value, preferred_element_type=jnp.float32).astype(jnp.bfloat16)
    heads_here = query.shape[1] // HEAD
    rows = query.shape[0]

    def by_head(x):
        return x.reshape(rows, heads_here, HEAD).transpose(1, 0, 2)

    context = attention(by_head(query), by_head(keys), by_head(values), dealt_ids)

    context_rows = lax.all_to_all(
        context.reshape(pages_dev, n_model, sub, head_cols),
        "mp",
        split_axis=1,
        concat_axis=1,
        tiled=True,
    )
    attended = jnp.zeros((pages_dev, sub, width), jnp.float32)
    for group in range(n_model):
        term = jnp.einsum(
            "pic,oc->pio",
            context_rows[:, group],
            out_all_t[:, group * head_cols : (group + 1) * head_cols],
            preferred_element_type=jnp.float32,
        ).astype(jnp.bfloat16)
        attended = attended + term.astype(jnp.float32)
    dealt_mine = lax.dynamic_index_in_dim(
        dealt.reshape(pages_dev, n_model, sub, width), me_model, axis=1, keepdims=False
    )
    first_mine = layer_norm(
        dealt_mine.astype(jnp.float32) + attended, gain_first, shift_first
    ).astype(jnp.bfloat16)
    hidden = jax.nn.gelu(
        jnp.einsum("pid,du->piu", first_mine, full_up, preferred_element_type=jnp.float32),
        approximate=False,
    ).astype(jnp.bfloat16)
    fed = jnp.zeros((pages_dev, sub, width), jnp.float32)
    for group in range(n_model):
        term = jnp.einsum(
            "piu,ou->pio",
            hidden[:, :, group * unit_part : (group + 1) * unit_part],
            down_t[:, group * unit_part : (group + 1) * unit_part],
            preferred_element_type=jnp.float32,
        ).astype(jnp.bfloat16)
        fed = fed + term.astype(jnp.float32)
    second_mine = layer_norm(first_mine.astype(jnp.float32) + fed, gain_second, shift_second).astype(
        jnp.bfloat16
    )

    valid = got_slots >= 0
    outgoing = jnp.where(
        valid[:, None, None],
        second_mine[jnp.clip(got_slots, 0, pages_dev - 1)],
        jnp.zeros((), second_mine.dtype),
    )
    returned = lax.all_to_all(outgoing, "dp", split_axis=0, concat_axis=0, tiled=True)
    mixed_mine = returned[position]
    mixed = lax.all_gather(mixed_mine, "mp", axis=1).reshape(pages_dev * page, width)
    kv_cache = jnp.stack([keys, values], axis=1)
    return (mixed, kv_cache)


def solution(mesh):
    return jax.shard_map(
        body,
        mesh=mesh,
        in_specs=(
            P("dp", None),
            P("dp"),
            P("dp"),
            P("dp", "mp"),
            P("dp", "mp"),
            P("dp", "mp"),
            P("mp", "dp"),
            P("dp", "mp"),
            P("mp", "dp"),
            P(),
            P(),
            P(),
            P(),
        ),
        out_specs=(P("dp", None), P("dp", None, "mp")),
        check_vma=False,
    )
```

```python
import jax
import jax.numpy as jnp
from jax import lax
from jax.experimental import pallas as pl
from jax.sharding import PartitionSpec as P

HEAD = 64


def layer_norm(hidden_sum, gain, shift):
    center = hidden_sum - jnp.mean(hidden_sum, axis=-1, keepdims=True)
    spread = jnp.mean(center * center, axis=-1, keepdims=True)
    return center * lax.rsqrt(spread + 1e-05) * gain + shift


def _attn_kernel(q_ref, k_ref, v_ref, qid_ref, kid_ref, o_ref):
    same = qid_ref[...] == kid_ref[...]
    for head in range(q_ref.shape[0]):
        scores = lax.dot_general(
            q_ref[head], k_ref[head], (((1,), (1,)), ((), ())), preferred_element_type=jnp.float32
        ) * (HEAD ** -0.5)
        scores = jnp.where(same, scores, -1e30)
        highest = jnp.max(scores, axis=1, keepdims=True)
        raised = jnp.exp(scores - highest)
        weights = (raised / jnp.sum(raised, axis=1, keepdims=True)).astype(jnp.bfloat16)
        o_ref[:, head * HEAD : (head + 1) * HEAD] = jnp.dot(
            weights, v_ref[head], preferred_element_type=jnp.float32
        ).astype(o_ref.dtype)


def attention(q, k, v, ids, block_q=256):
    heads, rows, dim = q.shape
    qid = ids.reshape(rows, 1)
    kid = ids.reshape(1, rows)
    return pl.pallas_call(
        _attn_kernel,
        out_shape=jax.ShapeDtypeStruct((rows, heads * dim), jnp.bfloat16),
        grid=(rows // block_q,),
        in_specs=[
            pl.BlockSpec((heads, block_q, dim), lambda i: (0, i, 0)),
            pl.BlockSpec((heads, rows, dim), lambda i: (0, 0, 0)),
            pl.BlockSpec((heads, rows, dim), lambda i: (0, 0, 0)),
            pl.BlockSpec((block_q, 1), lambda i: (i, 0)),
            pl.BlockSpec((1, rows), lambda i: (0, 0)),
        ],
        out_specs=pl.BlockSpec((block_q, heads * dim), lambda i: (i, 0)),
        cost_estimate=pl.CostEstimate(
            flops=4 * heads * rows * rows * dim,
            transcendentals=heads * rows * rows,
            bytes_accessed=4 * heads * rows * dim * 2,
        ),
    )(q, k, v, qid, kid)


def body(
    tokens,
    segment_ids,
    page_table,
    w_query,
    w_key,
    w_value,
    w_out,
    w_up,
    w_down,
    gain_first,
    shift_first,
    gain_second,
    shift_second,
):
    n_data = lax.axis_size("dp")
    n_model = lax.axis_size("mp")
    me_model = lax.axis_index("mp")
    pages_dev = page_table.shape[0]
    page = tokens.shape[0] // pages_dev
    width = tokens.shape[1]
    quarter = width // n_model
    sub = page // n_model
    slots_per = (pages_dev + n_data - 1) // n_data
    buffer_rows = n_data * slots_per

    head_cols = w_query.shape[1]
    in_part = w_out.shape[0]
    unit_part = w_up.shape[1]
    attn_local = jnp.concatenate([w_query, w_key, w_value], axis=1)
    attn_gathered = lax.all_gather(attn_local, "dp", axis=0, tiled=True)
    full_query = attn_gathered[:, :head_cols]
    full_key = attn_gathered[:, head_cols : 2 * head_cols]
    full_value = attn_gathered[:, 2 * head_cols : 3 * head_cols]
    small = jnp.concatenate([w_out.T, w_up, w_down.T], axis=1)

    target = page_table // pages_dev
    local_slot = page_table % pages_dev
    order = jnp.arange(pages_dev, dtype=jnp.int32)
    earlier = (target[:, None] == target[None, :]) & (order[:, None] < order[None, :])
    rank = jnp.sum(earlier.astype(jnp.int32), axis=0)
    position = target * slots_per + rank
    meta = jnp.zeros((pages_dev, 1, quarter), tokens.dtype)
    meta = meta.at[:, 0, :page].set(segment_ids.reshape(pages_dev, page).astype(tokens.dtype))
    meta = meta.at[:, 0, page].set(local_slot.astype(tokens.dtype))
    token_part = lax.dynamic_slice_in_dim(tokens, me_model * quarter, quarter, axis=1)
    token_pages = token_part.reshape(pages_dev, page, quarter)
    half = page // 2
    with_meta = jnp.concatenate([token_pages[:, :half], meta], axis=1)
    send_first = (
        jnp.zeros((buffer_rows, half + 1, quarter), tokens.dtype)
        .at[:, half, page]
        .set(-1)
        .at[position]
        .set(with_meta)
    )
    send_second = (
        jnp.zeros((buffer_rows, page - half, quarter), tokens.dtype)
        .at[position]
        .set(token_pages[:, half:])
    )
    got_first = lax.all_to_all(send_first, "dp", split_axis=0, concat_axis=0, tiled=True)
    got_ids = got_first[:, half, :page].astype(jnp.int32)
    got_slots = got_first[:, half, page].astype(jnp.int32)
    matches = got_slots[None, :] == order[:, None]
    source_row = jnp.sum(
        jnp.where(matches, jnp.arange(buffer_rows, dtype=jnp.int32)[None, :], 0), axis=1
    )
    dealt_first = got_first[:, :half][source_row]
    dealt_first, attn_gathered = lax.optimization_barrier((dealt_first, attn_gathered))
    dealt_first_all = lax.all_gather(dealt_first, "mp", axis=2, tiled=True)
    send_second, dealt_first = lax.optimization_barrier((send_second, dealt_first))
    got_second = lax.all_to_all(send_second, "dp", split_axis=0, concat_axis=0, tiled=True)
    dealt_second = got_second[source_row]
    small, dealt_second = lax.optimization_barrier((small, dealt_second))
    dealt_second_all = lax.all_gather(dealt_second, "mp", axis=2, tiled=True)
    small_all = lax.all_gather(small, "mp", axis=1)
    rows_dp = small.shape[0]
    out_rows = small_all[:, :, :in_part].reshape(rows_dp, n_model * in_part)
    up_rows = small_all[:, :, in_part : in_part + unit_part].reshape(rows_dp, n_model * unit_part)
    down_rows = small_all[:, :, in_part + unit_part :].reshape(rows_dp, n_model * unit_part)
    ffn_local = jnp.concatenate([out_rows, up_rows, down_rows], axis=1)
    dealt = jnp.concatenate([dealt_first_all, dealt_second_all], axis=1).reshape(
        pages_dev * page, width
    )
    dealt_ids = got_ids[source_row].reshape(pages_dev * page)
    ffn_local, dealt = lax.optimization_barrier((ffn_local, dealt))
    ffn_gathered = lax.all_gather(ffn_local, "dp", axis=0, tiled=True)
    units = n_model * unit_part
    in_all = n_model * in_part
    out_all_t = ffn_gathered[:, :in_all]
    full_up = ffn_gathered[:, in_all : in_all + units]
    down_t = ffn_gathered[:, in_all + units :]

    query = jnp.dot(dealt, full_query, preferred_element_type=jnp.float32).astype(jnp.bfloat16)
    keys = jnp.dot(dealt, full_key, preferred_element_type=jnp.float32).astype(jnp.bfloat16)
    values = jnp.dot(dealt, full_value, preferred_element_type=jnp.float32).astype(jnp.bfloat16)
    heads_here = query.shape[1] // HEAD
    rows = query.shape[0]

    def by_head(x):
        return x.reshape(rows, heads_here, HEAD).transpose(1, 0, 2)

    context = attention(by_head(query), by_head(keys), by_head(values), dealt_ids)

    context_rows = lax.all_to_all(
        context.reshape(pages_dev, n_model, sub, head_cols),
        "mp",
        split_axis=1,
        concat_axis=1,
        tiled=True,
    )
    attended = jnp.zeros((pages_dev, sub, width), jnp.float32)
    for group in range(n_model):
        term = jnp.einsum(
            "pic,oc->pio",
            context_rows[:, group],
            out_all_t[:, group * head_cols : (group + 1) * head_cols],
            preferred_element_type=jnp.float32,
        ).astype(jnp.bfloat16)
        attended = attended + term.astype(jnp.float32)
    dealt_mine = lax.dynamic_index_in_dim(
        dealt.reshape(pages_dev, n_model, sub, width), me_model, axis=1, keepdims=False
    )
    first_mine = layer_norm(
        dealt_mine.astype(jnp.float32) + attended, gain_first, shift_first
    ).astype(jnp.bfloat16)
    hidden = jax.nn.gelu(
        jnp.einsum("pid,du->piu", first_mine, full_up, preferred_element_type=jnp.float32),
        approximate=False,
    ).astype(jnp.bfloat16)
    fed = jnp.zeros((pages_dev, sub, width), jnp.float32)
    for group in range(n_model):
        term = jnp.einsum(
            "piu,ou->pio",
            hidden[:, :, group * unit_part : (group + 1) * unit_part],
            down_t[:, group * unit_part : (group + 1) * unit_part],
            preferred_element_type=jnp.float32,
        ).astype(jnp.bfloat16)
        fed = fed + term.astype(jnp.float32)
    second_mine = layer_norm(first_mine.astype(jnp.float32) + fed, gain_second, shift_second).astype(
        jnp.bfloat16
    )

    valid = got_slots >= 0
    outgoing = jnp.where(
        valid[:, None, None],
        second_mine[jnp.clip(got_slots, 0, pages_dev - 1)],
        jnp.zeros((), second_mine.dtype),
    )
    piece = sub // 2
    back_first = lax.all_to_all(outgoing[:, :piece], "dp", split_axis=0, concat_axis=0, tiled=True)
    back_second = lax.all_to_all(outgoing[:, piece:], "dp", split_axis=0, concat_axis=0, tiled=True)
    mixed_first = lax.all_gather(back_first[position], "mp", axis=1)
    mixed_second = lax.all_gather(back_second[position], "mp", axis=1)
    mixed = jnp.concatenate([mixed_first, mixed_second], axis=2).reshape(pages_dev * page, width)
    kv_cache = jnp.stack([keys, values], axis=1)
    return (mixed, kv_cache)


def solution(mesh):
    return jax.shard_map(
        body,
        mesh=mesh,
        in_specs=(
            P("dp", None),
            P("dp"),
            P("dp"),
            P("dp", "mp"),
            P("dp", "mp"),
            P("dp", "mp"),
            P("mp", "dp"),
            P("dp", "mp"),
            P("mp", "dp"),
            P(),
            P(),
            P(),
            P(),
        ),
        out_specs=(P("dp", None), P("dp", None, "mp")),
        check_vma=False,
    )
```

```python
import jax
import jax.numpy as jnp
from jax import lax
from jax.experimental import pallas as pl
from jax.sharding import PartitionSpec as P

HEAD = 64


def layer_norm(hidden_sum, gain, shift):
    center = hidden_sum - jnp.mean(hidden_sum, axis=-1, keepdims=True)
    spread = jnp.mean(center * center, axis=-1, keepdims=True)
    return center * lax.rsqrt(spread + 1e-05) * gain + shift


def _attn_kernel(q_ref, k_ref, v_ref, qid_ref, kid_ref, o_ref):
    same = qid_ref[...] == kid_ref[...]
    for head in range(q_ref.shape[0]):
        scores = lax.dot_general(
            q_ref[head], k_ref[head], (((1,), (1,)), ((), ())), preferred_element_type=jnp.float32
        ) * (HEAD ** -0.5)
        scores = jnp.where(same, scores, -1e30)
        highest = jnp.max(scores, axis=1, keepdims=True)
        raised = jnp.exp(scores - highest)
        weights = (raised / jnp.sum(raised, axis=1, keepdims=True)).astype(jnp.bfloat16)
        o_ref[:, head * HEAD : (head + 1) * HEAD] = jnp.dot(
            weights, v_ref[head], preferred_element_type=jnp.float32
        ).astype(o_ref.dtype)


def attention(q, k, v, ids, block_q=256):
    heads, rows, dim = q.shape
    qid = ids.reshape(rows, 1)
    kid = ids.reshape(1, rows)
    return pl.pallas_call(
        _attn_kernel,
        out_shape=jax.ShapeDtypeStruct((rows, heads * dim), jnp.bfloat16),
        grid=(rows // block_q,),
        in_specs=[
            pl.BlockSpec((heads, block_q, dim), lambda i: (0, i, 0)),
            pl.BlockSpec((heads, rows, dim), lambda i: (0, 0, 0)),
            pl.BlockSpec((heads, rows, dim), lambda i: (0, 0, 0)),
            pl.BlockSpec((block_q, 1), lambda i: (i, 0)),
            pl.BlockSpec((1, rows), lambda i: (0, 0)),
        ],
        out_specs=pl.BlockSpec((block_q, heads * dim), lambda i: (i, 0)),
        cost_estimate=pl.CostEstimate(
            flops=4 * heads * rows * rows * dim,
            transcendentals=heads * rows * rows,
            bytes_accessed=4 * heads * rows * dim * 2,
        ),
    )(q, k, v, qid, kid)


def body(
    tokens,
    segment_ids,
    page_table,
    w_query,
    w_key,
    w_value,
    w_out,
    w_up,
    w_down,
    gain_first,
    shift_first,
    gain_second,
    shift_second,
):
    n_data = lax.axis_size("dp")
    n_model = lax.axis_size("mp")
    me_model = lax.axis_index("mp")
    pages_dev = page_table.shape[0]
    page = tokens.shape[0] // pages_dev
    width = tokens.shape[1]
    quarter = width // n_model
    sub = page // n_model
    slots_per = (pages_dev + n_data - 1) // n_data
    buffer_rows = n_data * slots_per

    head_cols = w_query.shape[1]
    in_part = w_out.shape[0]
    unit_part = w_up.shape[1]
    attn_local = jnp.concatenate([w_query, w_key, w_value], axis=1)
    attn_gathered = lax.all_gather(attn_local, "dp", axis=0, tiled=True)
    full_query = attn_gathered[:, :head_cols]
    full_key = attn_gathered[:, head_cols : 2 * head_cols]
    full_value = attn_gathered[:, 2 * head_cols : 3 * head_cols]
    small = jnp.concatenate([w_out.T, w_up, w_down.T], axis=1)

    target = page_table // pages_dev
    local_slot = page_table % pages_dev
    order = jnp.arange(pages_dev, dtype=jnp.int32)
    earlier = (target[:, None] == target[None, :]) & (order[:, None] < order[None, :])
    rank = jnp.sum(earlier.astype(jnp.int32), axis=0)
    position = target * slots_per + rank
    meta = jnp.zeros((pages_dev, 1, quarter), tokens.dtype)
    meta = meta.at[:, 0, :page].set(segment_ids.reshape(pages_dev, page).astype(tokens.dtype))
    meta = meta.at[:, 0, page].set(local_slot.astype(tokens.dtype))
    token_part = lax.dynamic_slice_in_dim(tokens, me_model * quarter, quarter, axis=1)
    with_meta = jnp.concatenate([token_part.reshape(pages_dev, page, quarter), meta], axis=1)
    send_pages = (
        jnp.zeros((buffer_rows, page + 1, quarter), tokens.dtype)
        .at[:, page, page]
        .set(-1)
        .at[position]
        .set(with_meta)
    )
    small, send_pages = lax.optimization_barrier((small, send_pages))
    got_all = lax.all_to_all(send_pages, "dp", split_axis=0, concat_axis=0, tiled=True)
    got_pages = got_all[:, :page]
    got_ids = got_all[:, page, :page].astype(jnp.int32)
    got_slots = got_all[:, page, page].astype(jnp.int32)
    matches = got_slots[None, :] == order[:, None]
    source_row = jnp.sum(
        jnp.where(matches, jnp.arange(buffer_rows, dtype=jnp.int32)[None, :], 0), axis=1
    )
    small_all = lax.all_gather(small, "mp", axis=1)
    rows_dp = small.shape[0]
    out_rows = small_all[:, :, :in_part].reshape(rows_dp, n_model * in_part)
    up_rows = small_all[:, :, in_part : in_part + unit_part].reshape(rows_dp, n_model * unit_part)
    down_rows = small_all[:, :, in_part + unit_part :].reshape(rows_dp, n_model * unit_part)
    ffn_local = jnp.concatenate([out_rows, up_rows, down_rows], axis=1)
    dealt_part = got_pages[source_row]
    dealt_part, attn_gathered = lax.optimization_barrier((dealt_part, attn_gathered))
    dealt = lax.all_gather(dealt_part, "mp", axis=2, tiled=True).reshape(pages_dev * page, width)
    dealt_ids = got_ids[source_row].reshape(pages_dev * page)
    ffn_local, dealt = lax.optimization_barrier((ffn_local, dealt))
    ffn_gathered = lax.all_gather(ffn_local, "dp", axis=0, tiled=True)
    units = n_model * unit_part
    in_all = n_model * in_part
    out_all_t = ffn_gathered[:, :in_all]
    full_up = ffn_gathered[:, in_all : in_all + units]
    down_t = ffn_gathered[:, in_all + units :]

    query = jnp.dot(dealt, full_query, preferred_element_type=jnp.float32).astype(jnp.bfloat16)
    keys = jnp.dot(dealt, full_key, preferred_element_type=jnp.float32).astype(jnp.bfloat16)
    values = jnp.dot(dealt, full_value, preferred_element_type=jnp.float32).astype(jnp.bfloat16)
    heads_here = query.shape[1] // HEAD
    rows = query.shape[0]

    def by_head(x):
        return x.reshape(rows, heads_here, HEAD).transpose(1, 0, 2)

    context = attention(by_head(query), by_head(keys), by_head(values), dealt_ids)

    context_rows = lax.all_to_all(
        context.reshape(pages_dev, n_model, sub, head_cols),
        "mp",
        split_axis=1,
        concat_axis=1,
        tiled=True,
    )
    attended = jnp.zeros((pages_dev, sub, width), jnp.float32)
    for group in range(n_model):
        term = jnp.einsum(
            "pic,oc->pio",
            context_rows[:, group],
            out_all_t[:, group * head_cols : (group + 1) * head_cols],
            preferred_element_type=jnp.float32,
        ).astype(jnp.bfloat16)
        attended = attended + term.astype(jnp.float32)
    dealt_mine = lax.dynamic_index_in_dim(
        dealt.reshape(pages_dev, n_model, sub, width), me_model, axis=1, keepdims=False
    )
    first_mine = layer_norm(
        dealt_mine.astype(jnp.float32) + attended, gain_first, shift_first
    ).astype(jnp.bfloat16)
    hidden = jax.nn.gelu(
        jnp.einsum("pid,du->piu", first_mine, full_up, preferred_element_type=jnp.float32),
        approximate=False,
    ).astype(jnp.bfloat16)
    fed = jnp.zeros((pages_dev, sub, width), jnp.float32)
    for group in range(n_model):
        term = jnp.einsum(
            "piu,ou->pio",
            hidden[:, :, group * unit_part : (group + 1) * unit_part],
            down_t[:, group * unit_part : (group + 1) * unit_part],
            preferred_element_type=jnp.float32,
        ).astype(jnp.bfloat16)
        fed = fed + term.astype(jnp.float32)
    second_mine = layer_norm(first_mine.astype(jnp.float32) + fed, gain_second, shift_second).astype(
        jnp.bfloat16
    )

    valid = got_slots >= 0
    outgoing = jnp.where(
        valid[:, None, None],
        second_mine[jnp.clip(got_slots, 0, pages_dev - 1)],
        jnp.zeros((), second_mine.dtype),
    )
    returned = lax.all_to_all(outgoing, "dp", split_axis=0, concat_axis=0, tiled=True)
    mixed_mine = returned[position]
    mixed = lax.all_gather(mixed_mine, "mp", axis=1).reshape(pages_dev * page, width)
    kv_cache = jnp.stack([keys, values], axis=1)
    return (mixed, kv_cache)


def solution(mesh):
    return jax.shard_map(
        body,
        mesh=mesh,
        in_specs=(
            P("dp", None),
            P("dp"),
            P("dp"),
            P("dp", "mp"),
            P("dp", "mp"),
            P("dp", "mp"),
            P("mp", "dp"),
            P("dp", "mp"),
            P("mp", "dp"),
            P(),
            P(),
            P(),
            P(),
        ),
        out_specs=(P("dp", None), P("dp", None, "mp")),
        check_vma=False,
    )
```

```python
import jax
import jax.numpy as jnp
from jax import lax
from jax.experimental import pallas as pl
from jax.sharding import PartitionSpec as P

HEAD = 64


def layer_norm(hidden_sum, gain, shift):
    center = hidden_sum - jnp.mean(hidden_sum, axis=-1, keepdims=True)
    spread = jnp.mean(center * center, axis=-1, keepdims=True)
    return center * lax.rsqrt(spread + 1e-05) * gain + shift


def _attn_kernel(q_ref, k_ref, v_ref, qid_ref, kid_ref, o_ref):
    same = qid_ref[...] == kid_ref[...]
    for head in range(q_ref.shape[0]):
        scores = lax.dot_general(
            q_ref[head], k_ref[head], (((1,), (1,)), ((), ())), preferred_element_type=jnp.float32
        ) * (HEAD ** -0.5)
        scores = jnp.where(same, scores, -1e30)
        highest = jnp.max(scores, axis=1, keepdims=True)
        raised = jnp.exp(scores - highest)
        weights = (raised / jnp.sum(raised, axis=1, keepdims=True)).astype(jnp.bfloat16)
        o_ref[:, head * HEAD : (head + 1) * HEAD] = jnp.dot(
            weights, v_ref[head], preferred_element_type=jnp.float32
        ).astype(o_ref.dtype)


def attention(q, k, v, ids, block_q=256):
    heads, rows, dim = q.shape
    qid = ids.reshape(rows, 1)
    kid = ids.reshape(1, rows)
    return pl.pallas_call(
        _attn_kernel,
        out_shape=jax.ShapeDtypeStruct((rows, heads * dim), jnp.bfloat16),
        grid=(rows // block_q,),
        in_specs=[
            pl.BlockSpec((heads, block_q, dim), lambda i: (0, i, 0)),
            pl.BlockSpec((heads, rows, dim), lambda i: (0, 0, 0)),
            pl.BlockSpec((heads, rows, dim), lambda i: (0, 0, 0)),
            pl.BlockSpec((block_q, 1), lambda i: (i, 0)),
            pl.BlockSpec((1, rows), lambda i: (0, 0)),
        ],
        out_specs=pl.BlockSpec((block_q, heads * dim), lambda i: (i, 0)),
        cost_estimate=pl.CostEstimate(
            flops=4 * heads * rows * rows * dim,
            transcendentals=heads * rows * rows,
            bytes_accessed=4 * heads * rows * dim * 2,
        ),
    )(q, k, v, qid, kid)


def body(
    tokens,
    segment_ids,
    page_table,
    w_query,
    w_key,
    w_value,
    w_out,
    w_up,
    w_down,
    gain_first,
    shift_first,
    gain_second,
    shift_second,
):
    n_data = lax.axis_size("dp")
    n_model = lax.axis_size("mp")
    me_model = lax.axis_index("mp")
    pages_dev = page_table.shape[0]
    page = tokens.shape[0] // pages_dev
    width = tokens.shape[1]
    quarter = width // n_model
    sub = page // n_model
    slots_per = (pages_dev + n_data - 1) // n_data
    buffer_rows = n_data * slots_per

    head_cols = w_query.shape[1]
    in_part = w_out.shape[0]
    unit_part = w_up.shape[1]
    attn_local = jnp.concatenate([w_query, w_key, w_value], axis=1)
    attn_gathered = lax.all_gather(attn_local, "dp", axis=0, tiled=True)
    full_query = attn_gathered[:, :head_cols]
    full_key = attn_gathered[:, head_cols : 2 * head_cols]
    full_value = attn_gathered[:, 2 * head_cols : 3 * head_cols]
    small = jnp.concatenate([w_out.T, w_up, w_down.T], axis=1)

    target = page_table // pages_dev
    local_slot = page_table % pages_dev
    order = jnp.arange(pages_dev, dtype=jnp.int32)
    earlier = (target[:, None] == target[None, :]) & (order[:, None] < order[None, :])
    rank = jnp.sum(earlier.astype(jnp.int32), axis=0)
    position = target * slots_per + rank
    meta = jnp.zeros((pages_dev, 1, quarter), tokens.dtype)
    meta = meta.at[:, 0, :page].set(segment_ids.reshape(pages_dev, page).astype(tokens.dtype))
    meta = meta.at[:, 0, page].set(local_slot.astype(tokens.dtype))
    token_part = lax.dynamic_slice_in_dim(tokens, me_model * quarter, quarter, axis=1)
    with_meta = jnp.concatenate([token_part.reshape(pages_dev, page, quarter), meta], axis=1)
    send_pages = (
        jnp.zeros((buffer_rows, page + 1, quarter), tokens.dtype)
        .at[:, page, page]
        .set(-1)
        .at[position]
        .set(with_meta)
    )
    small, send_pages = lax.optimization_barrier((small, send_pages))
    got_all = lax.all_to_all(send_pages, "dp", split_axis=0, concat_axis=0, tiled=True)
    got_pages = got_all[:, :page]
    got_ids = got_all[:, page, :page].astype(jnp.int32)
    got_slots = got_all[:, page, page].astype(jnp.int32)
    matches = got_slots[None, :] == order[:, None]
    source_row = jnp.sum(
        jnp.where(matches, jnp.arange(buffer_rows, dtype=jnp.int32)[None, :], 0), axis=1
    )
    small_all = lax.all_gather(small, "mp", axis=1)
    rows_dp = small.shape[0]
    out_rows = small_all[:, :, :in_part].reshape(rows_dp, n_model * in_part)
    up_rows = small_all[:, :, in_part : in_part + unit_part].reshape(rows_dp, n_model * unit_part)
    down_rows = small_all[:, :, in_part + unit_part :].reshape(rows_dp, n_model * unit_part)
    ffn_local = jnp.concatenate([out_rows, up_rows, down_rows], axis=1)
    dealt_part = got_pages[source_row]
    dealt_part, attn_gathered = lax.optimization_barrier((dealt_part, attn_gathered))
    dealt = lax.all_gather(dealt_part, "mp", axis=2, tiled=True).reshape(pages_dev * page, width)
    dealt_ids = got_ids[source_row].reshape(pages_dev * page)
    ffn_local, dealt = lax.optimization_barrier((ffn_local, dealt))
    ffn_gathered = lax.all_gather(ffn_local, "dp", axis=0, tiled=True)
    units = n_model * unit_part
    in_all = n_model * in_part
    out_all_t = ffn_gathered[:, :in_all]
    full_up = ffn_gathered[:, in_all : in_all + units]
    down_t = ffn_gathered[:, in_all + units :]

    query = jnp.dot(dealt, full_query, preferred_element_type=jnp.float32).astype(jnp.bfloat16)
    keys = jnp.dot(dealt, full_key, preferred_element_type=jnp.float32).astype(jnp.bfloat16)
    values = jnp.dot(dealt, full_value, preferred_element_type=jnp.float32).astype(jnp.bfloat16)
    heads_here = query.shape[1] // HEAD
    rows = query.shape[0]

    def by_head(x):
        return x.reshape(rows, heads_here, HEAD).transpose(1, 0, 2)

    context = attention(by_head(query), by_head(keys), by_head(values), dealt_ids)

    context_rows = lax.all_to_all(
        context.reshape(pages_dev, n_model, sub, head_cols),
        "mp",
        split_axis=1,
        concat_axis=1,
        tiled=True,
    )
    attended = jnp.zeros((pages_dev, sub, width), jnp.float32)
    for group in range(n_model):
        term = jnp.einsum(
            "pic,oc->pio",
            context_rows[:, group],
            out_all_t[:, group * head_cols : (group + 1) * head_cols],
            preferred_element_type=jnp.float32,
        ).astype(jnp.bfloat16)
        attended = attended + term.astype(jnp.float32)
    dealt_mine = lax.dynamic_index_in_dim(
        dealt.reshape(pages_dev, n_model, sub, width), me_model, axis=1, keepdims=False
    )
    first_mine = layer_norm(
        dealt_mine.astype(jnp.float32) + attended, gain_first, shift_first
    ).astype(jnp.bfloat16)
    def feed_forward(first_rows):
        hidden = jax.nn.gelu(
            jnp.einsum("pid,du->piu", first_rows, full_up, preferred_element_type=jnp.float32),
            approximate=False,
        ).astype(jnp.bfloat16)
        fed = jnp.zeros(first_rows.shape, jnp.float32)
        for group in range(n_model):
            term = jnp.einsum(
                "piu,ou->pio",
                hidden[:, :, group * unit_part : (group + 1) * unit_part],
                down_t[:, group * unit_part : (group + 1) * unit_part],
                preferred_element_type=jnp.float32,
            ).astype(jnp.bfloat16)
            fed = fed + term.astype(jnp.float32)
        return layer_norm(
            first_rows.astype(jnp.float32) + fed, gain_second, shift_second
        ).astype(jnp.bfloat16)

    valid = got_slots >= 0
    piece = sub // 2
    pieces = []
    rest = first_mine[:, piece:]
    for at in (0, piece):
        if at == 0:
            second_rows = feed_forward(first_mine[:, :piece])
        else:
            rest, outgoing = lax.optimization_barrier((rest, outgoing))
            second_rows = feed_forward(rest)
        outgoing = jnp.where(
            valid[:, None, None],
            second_rows[jnp.clip(got_slots, 0, pages_dev - 1)],
            jnp.zeros((), second_rows.dtype),
        )
        returned = lax.all_to_all(outgoing, "dp", split_axis=0, concat_axis=0, tiled=True)
        pieces.append(returned[position])
    pieces = [lax.all_gather(part, "mp", axis=1) for part in pieces]
    mixed = jnp.concatenate(pieces, axis=2).reshape(pages_dev * page, width)
    kv_cache = jnp.stack([keys, values], axis=1)
    return (mixed, kv_cache)


def solution(mesh):
    return jax.shard_map(
        body,
        mesh=mesh,
        in_specs=(
            P("dp", None),
            P("dp"),
            P("dp"),
            P("dp", "mp"),
            P("dp", "mp"),
            P("dp", "mp"),
            P("mp", "dp"),
            P("dp", "mp"),
            P("mp", "dp"),
            P(),
            P(),
            P(),
            P(),
        ),
        out_specs=(P("dp", None), P("dp", None, "mp")),
        check_vma=False,
    )
```

```python
import jax
import jax.numpy as jnp
from jax import lax
from jax.experimental import pallas as pl
from jax.sharding import PartitionSpec as P

HEAD = 64


def layer_norm(hidden_sum, gain, shift):
    center = hidden_sum - jnp.mean(hidden_sum, axis=-1, keepdims=True)
    spread = jnp.mean(center * center, axis=-1, keepdims=True)
    return center * lax.rsqrt(spread + 1e-05) * gain + shift


def _attn_kernel(q_ref, k_ref, v_ref, qid_ref, kid_ref, o_ref):
    same = qid_ref[...] == kid_ref[...]
    for head in range(q_ref.shape[0]):
        scores = lax.dot_general(
            q_ref[head], k_ref[head], (((1,), (1,)), ((), ())), preferred_element_type=jnp.float32
        ) * (HEAD ** -0.5)
        scores = jnp.where(same, scores, -1e30)
        highest = jnp.max(scores, axis=1, keepdims=True)
        raised = jnp.exp(scores - highest)
        weights = (raised / jnp.sum(raised, axis=1, keepdims=True)).astype(jnp.bfloat16)
        o_ref[:, head * HEAD : (head + 1) * HEAD] = jnp.dot(
            weights, v_ref[head], preferred_element_type=jnp.float32
        ).astype(o_ref.dtype)


def attention(q, k, v, ids, block_q=256):
    heads, rows, dim = q.shape
    qid = ids.reshape(rows, 1)
    kid = ids.reshape(1, rows)
    return pl.pallas_call(
        _attn_kernel,
        out_shape=jax.ShapeDtypeStruct((rows, heads * dim), jnp.bfloat16),
        grid=(rows // block_q,),
        in_specs=[
            pl.BlockSpec((heads, block_q, dim), lambda i: (0, i, 0)),
            pl.BlockSpec((heads, rows, dim), lambda i: (0, 0, 0)),
            pl.BlockSpec((heads, rows, dim), lambda i: (0, 0, 0)),
            pl.BlockSpec((block_q, 1), lambda i: (i, 0)),
            pl.BlockSpec((1, rows), lambda i: (0, 0)),
        ],
        out_specs=pl.BlockSpec((block_q, heads * dim), lambda i: (i, 0)),
        cost_estimate=pl.CostEstimate(
            flops=4 * heads * rows * rows * dim,
            transcendentals=heads * rows * rows,
            bytes_accessed=4 * heads * rows * dim * 2,
        ),
    )(q, k, v, qid, kid)


def body(
    tokens,
    segment_ids,
    page_table,
    w_query,
    w_key,
    w_value,
    w_out,
    w_up,
    w_down,
    gain_first,
    shift_first,
    gain_second,
    shift_second,
):
    n_data = lax.axis_size("dp")
    n_model = lax.axis_size("mp")
    me_model = lax.axis_index("mp")
    pages_dev = page_table.shape[0]
    page = tokens.shape[0] // pages_dev
    width = tokens.shape[1]
    quarter = width // n_model
    sub = page // n_model
    slots_per = (pages_dev + n_data - 1) // n_data
    buffer_rows = n_data * slots_per

    head_cols = w_query.shape[1]
    in_part = w_out.shape[0]
    unit_part = w_up.shape[1]
    attn_local = jnp.concatenate([w_query, w_key, w_value], axis=1)
    attn_gathered = lax.all_gather(attn_local, "dp", axis=0, tiled=True)
    small = jnp.concatenate([w_out.T, w_up, w_down.T], axis=1)

    target = page_table // pages_dev
    local_slot = page_table % pages_dev
    order = jnp.arange(pages_dev, dtype=jnp.int32)
    earlier = (target[:, None] == target[None, :]) & (order[:, None] < order[None, :])
    rank = jnp.sum(earlier.astype(jnp.int32), axis=0)
    position = target * slots_per + rank
    meta = jnp.zeros((pages_dev, 1, quarter), tokens.dtype)
    meta = meta.at[:, 0, :page].set(segment_ids.reshape(pages_dev, page).astype(tokens.dtype))
    meta = meta.at[:, 0, page].set(local_slot.astype(tokens.dtype))
    token_part = lax.dynamic_slice_in_dim(tokens, me_model * quarter, quarter, axis=1)
    with_meta = jnp.concatenate([token_part.reshape(pages_dev, page, quarter), meta], axis=1)
    send_pages = (
        jnp.zeros((buffer_rows, page + 1, quarter), tokens.dtype)
        .at[:, page, page]
        .set(-1)
        .at[position]
        .set(with_meta)
    )
    small, send_pages = lax.optimization_barrier((small, send_pages))
    got_all = lax.all_to_all(send_pages, "dp", split_axis=0, concat_axis=0, tiled=True)
    got_pages = got_all[:, :page]
    got_ids = got_all[:, page, :page].astype(jnp.int32)
    got_slots = got_all[:, page, page].astype(jnp.int32)
    matches = got_slots[None, :] == order[:, None]
    source_row = jnp.sum(
        jnp.where(matches, jnp.arange(buffer_rows, dtype=jnp.int32)[None, :], 0), axis=1
    )
    small_all = lax.all_gather(small, "mp", axis=1)
    rows_dp = small.shape[0]
    out_rows = small_all[:, :, :in_part].reshape(rows_dp, n_model * in_part)
    up_rows = small_all[:, :, in_part : in_part + unit_part].reshape(rows_dp, n_model * unit_part)
    down_rows = small_all[:, :, in_part + unit_part :].reshape(rows_dp, n_model * unit_part)
    ffn_local = jnp.concatenate([out_rows, up_rows, down_rows], axis=1)
    dealt_part = got_pages[source_row]
    dealt_part, attn_gathered = lax.optimization_barrier((dealt_part, attn_gathered))
    dealt = lax.all_gather(dealt_part, "mp", axis=2, tiled=True).reshape(pages_dev * page, width)
    dealt_ids = got_ids[source_row].reshape(pages_dev * page)
    ffn_local, dealt = lax.optimization_barrier((ffn_local, dealt))
    ffn_gathered = lax.all_gather(ffn_local, "dp", axis=0, tiled=True)
    units = n_model * unit_part
    in_all = n_model * in_part
    out_all_t = ffn_gathered[:, :in_all]
    full_up = ffn_gathered[:, in_all : in_all + units]
    down_t = ffn_gathered[:, in_all + units :]

    projected = jnp.dot(dealt, attn_gathered, preferred_element_type=jnp.float32).astype(
        jnp.bfloat16
    )
    keys = projected[:, head_cols : 2 * head_cols]
    values = projected[:, 2 * head_cols :]
    heads_here = head_cols // HEAD
    rows = projected.shape[0]
    by_head = projected.reshape(rows, 3 * heads_here, HEAD).transpose(1, 0, 2)
    context = attention(
        by_head[:heads_here],
        by_head[heads_here : 2 * heads_here],
        by_head[2 * heads_here :],
        dealt_ids,
    )

    context_rows = lax.all_to_all(
        context.reshape(pages_dev, n_model, sub, head_cols),
        "mp",
        split_axis=1,
        concat_axis=1,
        tiled=True,
    )
    attended = jnp.zeros((pages_dev, sub, width), jnp.float32)
    for group in range(n_model):
        term = jnp.einsum(
            "pic,oc->pio",
            context_rows[:, group],
            out_all_t[:, group * head_cols : (group + 1) * head_cols],
            preferred_element_type=jnp.float32,
        ).astype(jnp.bfloat16)
        attended = attended + term.astype(jnp.float32)
    dealt_mine = lax.dynamic_index_in_dim(
        dealt.reshape(pages_dev, n_model, sub, width), me_model, axis=1, keepdims=False
    )
    first_mine = layer_norm(
        dealt_mine.astype(jnp.float32) + attended, gain_first, shift_first
    ).astype(jnp.bfloat16)
    def feed_forward(first_rows):
        hidden = jax.nn.gelu(
            jnp.einsum("pid,du->piu", first_rows, full_up, preferred_element_type=jnp.float32),
            approximate=False,
        ).astype(jnp.bfloat16)
        fed = jnp.zeros(first_rows.shape, jnp.float32)
        for group in range(n_model):
            term = jnp.einsum(
                "piu,ou->pio",
                hidden[:, :, group * unit_part : (group + 1) * unit_part],
                down_t[:, group * unit_part : (group + 1) * unit_part],
                preferred_element_type=jnp.float32,
            ).astype(jnp.bfloat16)
            fed = fed + term.astype(jnp.float32)
        return layer_norm(
            first_rows.astype(jnp.float32) + fed, gain_second, shift_second
        ).astype(jnp.bfloat16)

    valid = got_slots >= 0
    piece = sub // 2
    pieces = []
    rest = first_mine[:, piece:]
    for at in (0, piece):
        if at == 0:
            second_rows = feed_forward(first_mine[:, :piece])
        else:
            rest, outgoing = lax.optimization_barrier((rest, outgoing))
            second_rows = feed_forward(rest)
        outgoing = jnp.where(
            valid[:, None, None],
            second_rows[jnp.clip(got_slots, 0, pages_dev - 1)],
            jnp.zeros((), second_rows.dtype),
        )
        returned = lax.all_to_all(outgoing, "dp", split_axis=0, concat_axis=0, tiled=True)
        pieces.append(returned[position])
    pieces = [lax.all_gather(part, "mp", axis=1) for part in pieces]
    mixed = jnp.concatenate(pieces, axis=2).reshape(pages_dev * page, width)
    kv_cache = jnp.stack([keys, values], axis=1)
    return (mixed, kv_cache)


def solution(mesh):
    return jax.shard_map(
        body,
        mesh=mesh,
        in_specs=(
            P("dp", None),
            P("dp"),
            P("dp"),
            P("dp", "mp"),
            P("dp", "mp"),
            P("dp", "mp"),
            P("mp", "dp"),
            P("dp", "mp"),
            P("mp", "dp"),
            P(),
            P(),
            P(),
            P(),
        ),
        out_specs=(P("dp", None), P("dp", None, "mp")),
        check_vma=False,
    )
```

```python
import jax
import jax.numpy as jnp
from jax import lax
from jax.experimental import pallas as pl
from jax.experimental.pallas import tpu as pltpu
from jax.sharding import PartitionSpec as P

HEAD = 64


def layer_norm(hidden_sum, gain, shift):
    center = hidden_sum - jnp.mean(hidden_sum, axis=-1, keepdims=True)
    spread = jnp.mean(center * center, axis=-1, keepdims=True)
    return center * lax.rsqrt(spread + 1e-05) * gain + shift


KEY_CHUNK = 256


def _attn_kernel(lo_ref, hi_ref, q_ref, k_ref, v_ref, qid_ref, kid_ref, o_ref, s_ref, m_ref, l_ref, acc_ref):
    block = pl.program_id(0)
    lo = lo_ref[block]
    hi = hi_ref[block]
    chunks = k_ref.shape[1] // KEY_CHUNK
    qid = qid_ref[...]
    for head in range(q_ref.shape[0]):
        q = q_ref[head]
        m_ref[...] = jnp.full(m_ref.shape, -jnp.inf, jnp.float32)
        l_ref[...] = jnp.zeros(l_ref.shape, jnp.float32)
        acc_ref[...] = jnp.zeros(acc_ref.shape, jnp.float32)
        for c in range(chunks):
            cols = slice(c * KEY_CHUNK, (c + 1) * KEY_CHUNK)

            @pl.when((c >= lo) & (c < hi))
            def _():
                scores = lax.dot_general(
                    q, k_ref[head, cols, :], (((1,), (1,)), ((), ())),
                    preferred_element_type=jnp.float32,
                ) * (HEAD ** -0.5)
                scores = jnp.where(qid == kid_ref[:, cols], scores, -1e30)
                s_ref[:, cols] = scores
                m_ref[...] = jnp.maximum(m_ref[...], jnp.max(scores, axis=1, keepdims=True))

        for c in range(chunks):
            cols = slice(c * KEY_CHUNK, (c + 1) * KEY_CHUNK)

            @pl.when((c >= lo) & (c < hi))
            def _():
                raised = jnp.exp(s_ref[:, cols] - m_ref[...])
                s_ref[:, cols] = raised
                l_ref[...] = l_ref[...] + jnp.sum(raised, axis=1, keepdims=True)

        for c in range(chunks):
            cols = slice(c * KEY_CHUNK, (c + 1) * KEY_CHUNK)

            @pl.when((c >= lo) & (c < hi))
            def _():
                weights = (s_ref[:, cols] / l_ref[...]).astype(jnp.bfloat16)
                acc_ref[...] = acc_ref[...] + jnp.dot(
                    weights, v_ref[head, cols, :], preferred_element_type=jnp.float32
                )

        o_ref[:, head * HEAD : (head + 1) * HEAD] = acc_ref[...].astype(o_ref.dtype)


def key_ranges(ids, block_q):
    rows = ids.shape[0]
    index = jnp.arange(rows, dtype=jnp.int32)
    new_run = jnp.concatenate([jnp.ones((1,), bool), ids[1:] != ids[:-1]])
    run_start = lax.cummax(jnp.where(new_run, index, 0))
    run_last = jnp.concatenate([ids[1:] != ids[:-1], jnp.ones((1,), bool)])
    run_end = lax.cummin(jnp.where(run_last, index + 1, rows), reverse=True)
    lo = run_start[::block_q] // KEY_CHUNK
    hi = (run_end[block_q - 1 :: block_q] + KEY_CHUNK - 1) // KEY_CHUNK
    return lo.astype(jnp.int32), hi.astype(jnp.int32)


def attention(q, k, v, ids, block_q=256):
    heads, rows, dim = q.shape
    lo, hi = key_ranges(ids, block_q)
    qid = ids.reshape(rows, 1)
    kid = ids.reshape(1, rows)
    return pl.pallas_call(
        _attn_kernel,
        out_shape=jax.ShapeDtypeStruct((rows, heads * dim), jnp.bfloat16),
        grid_spec=pltpu.PrefetchScalarGridSpec(
            num_scalar_prefetch=2,
            grid=(rows // block_q,),
            in_specs=[
                pl.BlockSpec((heads, block_q, dim), lambda i, lo, hi: (0, i, 0)),
                pl.BlockSpec((heads, rows, dim), lambda i, lo, hi: (0, 0, 0)),
                pl.BlockSpec((heads, rows, dim), lambda i, lo, hi: (0, 0, 0)),
                pl.BlockSpec((block_q, 1), lambda i, lo, hi: (i, 0)),
                pl.BlockSpec((1, rows), lambda i, lo, hi: (0, 0)),
            ],
            out_specs=pl.BlockSpec((block_q, heads * dim), lambda i, lo, hi: (i, 0)),
            scratch_shapes=[
                pltpu.VMEM((block_q, rows), jnp.float32),
                pltpu.VMEM((block_q, 1), jnp.float32),
                pltpu.VMEM((block_q, 1), jnp.float32),
                pltpu.VMEM((block_q, dim), jnp.float32),
            ],
        ),
        cost_estimate=pl.CostEstimate(
            flops=2 * heads * rows * rows * dim,
            transcendentals=heads * rows * rows // 2,
            bytes_accessed=4 * heads * rows * dim * 2,
        ),
    )(lo, hi, q, k, v, qid, kid)


def body(
    tokens,
    segment_ids,
    page_table,
    w_query,
    w_key,
    w_value,
    w_out,
    w_up,
    w_down,
    gain_first,
    shift_first,
    gain_second,
    shift_second,
):
    n_data = lax.axis_size("dp")
    n_model = lax.axis_size("mp")
    me_model = lax.axis_index("mp")
    pages_dev = page_table.shape[0]
    page = tokens.shape[0] // pages_dev
    width = tokens.shape[1]
    quarter = width // n_model
    sub = page // n_model
    slots_per = (pages_dev + n_data - 1) // n_data
    buffer_rows = n_data * slots_per

    head_cols = w_query.shape[1]
    in_part = w_out.shape[0]
    unit_part = w_up.shape[1]
    attn_local = jnp.concatenate([w_query, w_key, w_value], axis=1)
    attn_gathered = lax.all_gather(attn_local, "dp", axis=0, tiled=True)
    full_query = attn_gathered[:, :head_cols]
    full_key = attn_gathered[:, head_cols : 2 * head_cols]
    full_value = attn_gathered[:, 2 * head_cols : 3 * head_cols]
    small = jnp.concatenate([w_out.T, w_up, w_down.T], axis=1)

    target = page_table // pages_dev
    local_slot = page_table % pages_dev
    order = jnp.arange(pages_dev, dtype=jnp.int32)
    earlier = (target[:, None] == target[None, :]) & (order[:, None] < order[None, :])
    rank = jnp.sum(earlier.astype(jnp.int32), axis=0)
    position = target * slots_per + rank
    meta = jnp.zeros((pages_dev, 1, quarter), tokens.dtype)
    meta = meta.at[:, 0, :page].set(segment_ids.reshape(pages_dev, page).astype(tokens.dtype))
    meta = meta.at[:, 0, page].set(local_slot.astype(tokens.dtype))
    token_part = lax.dynamic_slice_in_dim(tokens, me_model * quarter, quarter, axis=1)
    with_meta = jnp.concatenate([token_part.reshape(pages_dev, page, quarter), meta], axis=1)
    send_pages = (
        jnp.zeros((buffer_rows, page + 1, quarter), tokens.dtype)
        .at[:, page, page]
        .set(-1)
        .at[position]
        .set(with_meta)
    )
    small, send_pages = lax.optimization_barrier((small, send_pages))
    got_all = lax.all_to_all(send_pages, "dp", split_axis=0, concat_axis=0, tiled=True)
    got_pages = got_all[:, :page]
    got_ids = got_all[:, page, :page].astype(jnp.int32)
    got_slots = got_all[:, page, page].astype(jnp.int32)
    matches = got_slots[None, :] == order[:, None]
    source_row = jnp.sum(
        jnp.where(matches, jnp.arange(buffer_rows, dtype=jnp.int32)[None, :], 0), axis=1
    )
    small_all = lax.all_gather(small, "mp", axis=1)
    rows_dp = small.shape[0]
    out_rows = small_all[:, :, :in_part].reshape(rows_dp, n_model * in_part)
    up_rows = small_all[:, :, in_part : in_part + unit_part].reshape(rows_dp, n_model * unit_part)
    down_rows = small_all[:, :, in_part + unit_part :].reshape(rows_dp, n_model * unit_part)
    ffn_local = jnp.concatenate([out_rows, up_rows, down_rows], axis=1)
    dealt_part = got_pages[source_row]
    dealt_part, attn_gathered = lax.optimization_barrier((dealt_part, attn_gathered))
    dealt = lax.all_gather(dealt_part, "mp", axis=2, tiled=True).reshape(pages_dev * page, width)
    dealt_ids = got_ids[source_row].reshape(pages_dev * page)
    ffn_local, dealt = lax.optimization_barrier((ffn_local, dealt))
    ffn_gathered = lax.all_gather(ffn_local, "dp", axis=0, tiled=True)
    units = n_model * unit_part
    in_all = n_model * in_part
    out_all_t = ffn_gathered[:, :in_all]
    full_up = ffn_gathered[:, in_all : in_all + units]
    down_t = ffn_gathered[:, in_all + units :]

    query = jnp.dot(dealt, full_query, preferred_element_type=jnp.float32).astype(jnp.bfloat16)
    keys = jnp.dot(dealt, full_key, preferred_element_type=jnp.float32).astype(jnp.bfloat16)
    values = jnp.dot(dealt, full_value, preferred_element_type=jnp.float32).astype(jnp.bfloat16)
    heads_here = query.shape[1] // HEAD
    rows = query.shape[0]

    def by_head(x):
        return x.reshape(rows, heads_here, HEAD).transpose(1, 0, 2)

    context = attention(by_head(query), by_head(keys), by_head(values), dealt_ids)

    context_rows = lax.all_to_all(
        context.reshape(pages_dev, n_model, sub, head_cols),
        "mp",
        split_axis=1,
        concat_axis=1,
        tiled=True,
    )
    attended = jnp.zeros((pages_dev, sub, width), jnp.float32)
    for group in range(n_model):
        term = jnp.einsum(
            "pic,oc->pio",
            context_rows[:, group],
            out_all_t[:, group * head_cols : (group + 1) * head_cols],
            preferred_element_type=jnp.float32,
        ).astype(jnp.bfloat16)
        attended = attended + term.astype(jnp.float32)
    dealt_mine = lax.dynamic_index_in_dim(
        dealt.reshape(pages_dev, n_model, sub, width), me_model, axis=1, keepdims=False
    )
    first_mine = layer_norm(
        dealt_mine.astype(jnp.float32) + attended, gain_first, shift_first
    ).astype(jnp.bfloat16)
    def feed_forward(first_rows):
        hidden = jax.nn.gelu(
            jnp.einsum("pid,du->piu", first_rows, full_up, preferred_element_type=jnp.float32),
            approximate=False,
        ).astype(jnp.bfloat16)
        fed = jnp.zeros(first_rows.shape, jnp.float32)
        for group in range(n_model):
            term = jnp.einsum(
                "piu,ou->pio",
                hidden[:, :, group * unit_part : (group + 1) * unit_part],
                down_t[:, group * unit_part : (group + 1) * unit_part],
                preferred_element_type=jnp.float32,
            ).astype(jnp.bfloat16)
            fed = fed + term.astype(jnp.float32)
        return layer_norm(
            first_rows.astype(jnp.float32) + fed, gain_second, shift_second
        ).astype(jnp.bfloat16)

    valid = got_slots >= 0
    piece = sub // 2
    pieces = []
    rest = first_mine[:, piece:]
    for at in (0, piece):
        if at == 0:
            second_rows = feed_forward(first_mine[:, :piece])
        else:
            rest, outgoing = lax.optimization_barrier((rest, outgoing))
            second_rows = feed_forward(rest)
        outgoing = jnp.where(
            valid[:, None, None],
            second_rows[jnp.clip(got_slots, 0, pages_dev - 1)],
            jnp.zeros((), second_rows.dtype),
        )
        returned = lax.all_to_all(outgoing, "dp", split_axis=0, concat_axis=0, tiled=True)
        pieces.append(returned[position])
    pieces = [lax.all_gather(part, "mp", axis=1) for part in pieces]
    mixed = jnp.concatenate(pieces, axis=2).reshape(pages_dev * page, width)
    kv_cache = jnp.stack([keys, values], axis=1)
    return (mixed, kv_cache)


def solution(mesh):
    return jax.shard_map(
        body,
        mesh=mesh,
        in_specs=(
            P("dp", None),
            P("dp"),
            P("dp"),
            P("dp", "mp"),
            P("dp", "mp"),
            P("dp", "mp"),
            P("mp", "dp"),
            P("dp", "mp"),
            P("mp", "dp"),
            P(),
            P(),
            P(),
            P(),
        ),
        out_specs=(P("dp", None), P("dp", None, "mp")),
        check_vma=False,
    )
```
